128 devices in a mesh: req: 32 (over x, z, core), tp: 4 (over y).
Axes of the slice: x: 4, y: 4, z: 4, core: 2. Of those that a mesh axis runs over, the one named last changes fastest.
Arguments:
- hidden: bfloat16 [8192, 2048], P('req', 'tp'), may hold values from -45 to 45
- routes: int32 [8192, 2], P('req'), may hold values from 0 to 7, all different within a row; in each aligned block of 256 rows (0 to 255, 256 to 511, ...) at most 128 rows name the same one
- route_weights: float32 [8192, 2], P('req'), may hold values from 0.2 to 1
- pre_gain: float32 [2048], replicated, may hold values from 0.1 to 1.9
- out_gain: float32 [2048], P('tp'), may hold values from 0.1 to 1.9
- gate_weight: bfloat16 [32, 2048, 5632], P('req', None, 'tp'), as said below
- up_weight: bfloat16 [32, 2048, 5632], P('req', None, 'tp'), as said below
- down_weight: bfloat16 [32, 5632, 2048], P('req', 'tp'), as said below
Outputs:
- residual_out: bfloat16 [8192, 2048], P('req', 'tp')
- normed_out: bfloat16 [8192, 2048], P('req', 'tp')
The draws below stay inside these ranges and needn't reach their ends.
Inputs may be any that keep to these rules, and one draw needn't show every extreme that they name: `routes`: each row names 2 different experts; in the rows of one index of req no expert is named by more than 128 rows, a bound that some block reaches. `gate_weight`: index r holds expert r % 8. `up_weight`: index r holds expert r % 8. `down_weight`: index r holds expert r % 8.
All inputs are finite; a program needn't handle non-finite values.
Results may differ from the reference program's by a relative error of at most 0.007.
Values may be sent and summed in bfloat16 or wider, within the bound.
No kernel may reach another device: no remote copies, remote signals or barrier semaphores. Data moves between devices by JAX's collectives and lax.ppermute only.
A program may use at most 128 MiB of HBM per device.

```python
import math
import jax
import jax.numpy as jnp
import numpy as np
from jax import lax

D = 2048
FF = 5632
E = 8
TOP = 2
TOK_DEV = 256
CAP = 128
COPIES = 4
ROWS = 8192
N_REQ = 32
N_TP = 4


def draw_hidden(key, part):
    key_a, key_b = jax.random.split(jax.random.fold_in(key, 5))
    col_scale = 0.3 * 10.0 ** (jnp.arange(D, dtype=jnp.float32) / (D - 1))
    noise = jnp.clip(jax.random.normal(key_a, (ROWS, D), jnp.float32), -5.0, 5.0)
    row_scale = jnp.exp(jax.random.uniform(key_b, (ROWS, 1), jnp.float32, math.log(0.3), math.log(3.0)))
    return (noise * row_scale * col_scale[None, :]).astype(jnp.bfloat16)


def tiled_weight(key, rows_in, cols_out):
    base = jnp.clip(jax.random.normal(key, (E, rows_in, cols_out), jnp.float32), -6.0, 6.0) * rows_in ** (-0.5)
    return jnp.tile(base, (COPIES, 1, 1)).astype(jnp.bfloat16)


def draw_gate_weight(key, part):
    return tiled_weight(jax.random.fold_in(key, 11), D, FF)


def draw_up_weight(key, part):
    return tiled_weight(jax.random.fold_in(key, 12), D, FF)


def draw_down_weight(key, part):
    return tiled_weight(jax.random.fold_in(key, 13), FF, D)


def level_of(key, shape, cuts, low, top_value):
    factor_of, own = 1.0, jax.random.fold_in(key, 6)
    for dim, parts in cuts:
        draws = jnp.exp(jax.random.uniform(jax.random.fold_in(own, dim), (parts,), jnp.float32, low / len(cuts), top_value / len(cuts)))
        factor_of = factor_of * jnp.repeat(draws, shape[dim] // parts).reshape([-1 if axis == dim else 1 for axis in range(len(shape))])
    return factor_of


def assign_block(key, own, number, rows, amount, top, limit, skew):
    ranking = jax.random.permutation(key, amount)
    crowded, usual = shares(amount, rows * top, limit, skew, True), shares(amount, rows * top, limit, skew, False)
    places = jnp.arange(amount)

    def named(lengths, turn):
        used = int((lengths > 0).sum())
        fixed = max(1, used // 4)
        passed = fixed + (places - fixed + turn * (used - fixed)) % max(1, amount - fixed)
        return jnp.zeros((amount,), jnp.int32).at[ranking[jnp.where(places < fixed, places, passed)]].set(jnp.asarray(lengths, jnp.int32))

    lengths = jnp.where(number % 4 == 0, named(crowded, number // 4), named(usual, number - number // 4 - 1))
    mixed = jax.random.permutation(jax.random.fold_in(own, 3), amount)
    giver, sink = mixed[0:amount // 2 * 2:2], mixed[1:amount // 2 * 2:2]
    margin = jnp.minimum(lengths[giver] - 1, limit - lengths[sink]) // 2
    margin = jnp.where((giver == ranking[0]) | (sink == ranking[0]) | (lengths[sink] == 0), 0, jnp.maximum(margin, 0))
    passed = jax.random.randint(jax.random.fold_in(own, 4), (amount // 2,), 0, 1 << 20) % (margin + 1)
    lengths = lengths.at[giver].add(-passed).at[sink].add(passed)
    members = jnp.searchsorted(jnp.cumsum(lengths), jnp.arange(rows * top), side="right").astype(jnp.int32)
    table = members.reshape(top, rows).T
    table = table[jax.random.permutation(jax.random.fold_in(own, 1), rows)]
    turn = jax.random.randint(jax.random.fold_in(own, 2), (rows, 1), 0, top)
    return jnp.take_along_axis(table, (jnp.arange(top)[None, :] + turn) % top, axis=1)


def shares(count, total, bound, skew, full):
    loads = [(1 << 20) // math.isqrt(grade ** skew) + 1 for grade in range(1, count + 1)]
    largest = bound if full else min(bound, max(-(-total // count), total * loads[0] // sum(loads)))
    least = 1 if total - largest >= count - 1 else 0
    given, rest = [largest] + [least] * (count - 1), total - largest - least * (count - 1)
    while rest > 0:
        candidates = [i for i in range(1, count) if given[i] < largest] or [i for i in range(1, count) if given[i] < bound]
        mass, budget = sum([loads[i] for i in candidates]), rest
        for i in candidates:
            addition = min(bound - given[i], max(1, budget * loads[i] // mass), rest)
            given[i] = given[i] + addition
            rest = rest - addition
    return np.array(given)


def setup_inputs(seed: int = 0) -> dict:
    keys = jax.random.split(jax.random.key(seed), 9)
    hidden = draw_hidden(jax.random.fold_in(keys[8], 71), 0)
    routes_keys = jax.random.split(jax.random.fold_in(keys[1], 1), ROWS // TOK_DEV)
    routes_turns = jax.random.permutation(jax.random.fold_in(keys[1], 3), ROWS // TOK_DEV)
    routes = jax.vmap(lambda own, number: assign_block(jax.random.fold_in(keys[1], 2), own, number, TOK_DEV, E, TOP, CAP, 1))(routes_keys, routes_turns).reshape((ROWS, TOP))
    route_weights = jnp.clip(0.2 + 0.8 * jax.random.uniform(keys[2], (ROWS, TOP), jnp.float32) ** level_of(keys[2], (ROWS, TOP), ((0, 32),), -0.2, 0.2), 0.2, 1.0)
    pre_gain = jnp.clip(1.0 + 0.18 * jax.random.normal(keys[3], (D,), jnp.float32), 0.1, 1.9)
    out_gain = jnp.clip(1.0 + 0.18 * jax.random.normal(keys[4], (D,), jnp.float32), 0.1, 1.9)
    gate_weight = draw_gate_weight(jax.random.fold_in(keys[8], 71), 0)
    up_weight = draw_up_weight(jax.random.fold_in(keys[8], 71), 0)
    down_weight = draw_down_weight(jax.random.fold_in(keys[8], 71), 0)
    return {"hidden": hidden, "routes": routes, "route_weights": route_weights, "pre_gain": pre_gain, "out_gain": out_gain, "gate_weight": gate_weight, "up_weight": up_weight, "down_weight": down_weight}


epsilon = 1e-05

def rms_scale(values, gain_vec):
    meansq = lax.optimization_barrier(jnp.mean(values * values, axis=-1, keepdims=True))
    return values * lax.rsqrt(meansq + epsilon) * gain_vec.astype(jnp.float32)

def reference(hidden, routes, route_weights, pre_gain, out_gain, gate_weight, up_weight, down_weight):
    stream = hidden.astype(jnp.float32)
    normed_in = rms_scale(stream, pre_gain).astype(jnp.bfloat16)
    chosen = routes.reshape(N_REQ, TOP * TOK_DEV).astype(jnp.int32)
    onehot = (chosen[:, :, None] == jnp.arange(E, dtype=jnp.int32)[None, None, :]).astype(jnp.int32)
    slot_rank = lax.optimization_barrier(jnp.sum((jnp.cumsum(onehot, axis=1) - 1) * onehot, axis=2)).astype(jnp.int32)
    device_col = jnp.arange(N_REQ, dtype=jnp.int32)[:, None]
    column = (device_col * CAP + slot_rank).astype(jnp.int32)
    row_ids = (device_col * TOK_DEV + jnp.arange(TOP * TOK_DEV, dtype=jnp.int32)[None, :] // TOP).astype(jnp.int32)
    table = jnp.zeros((E, N_REQ * CAP), jnp.int32).at[chosen, column].set(row_ids)
    shard_len = FF // N_TP

    def expert_rows(inputs):
        indices, w_gate, w_up, w_down = inputs
        gathered = normed_in[indices]
        gate_val = jnp.dot(gathered, w_gate, preferred_element_type=jnp.float32)
        up_val = jnp.dot(gathered, w_up, preferred_element_type=jnp.float32)
        activ = (jax.nn.silu(gate_val) * up_val).astype(jnp.bfloat16)
        total = jnp.zeros((indices.shape[0], D), jnp.float32)
        for shard in range(N_TP):
            term = jnp.dot(activ[:, shard * shard_len:(shard + 1) * shard_len], w_down[shard * shard_len:(shard + 1) * shard_len], preferred_element_type=jnp.float32)
            total = total + lax.optimization_barrier(term.astype(jnp.bfloat16)).astype(jnp.float32)
        return total.astype(jnp.bfloat16)
    results = lax.map(expert_rows, (table, gate_weight[:E], up_weight[:E], down_weight[:E]))
    picked = results[chosen, column].reshape(N_REQ * TOK_DEV, TOP, D).astype(jnp.float32)
    mixed = lax.optimization_barrier(jnp.sum(picked * route_weights.astype(jnp.float32)[:, :, None], axis=1))
    total_stream = stream + mixed
    return (total_stream.astype(jnp.bfloat16), rms_scale(total_stream, out_gain).astype(jnp.bfloat16))
```

```python
import jax
import jax.numpy as jnp
from jax import lax
from jax.sharding import PartitionSpec as P

E = 8
CAP = 128


epsilon = 1e-05


def shards(hidden, routes, route_weights, pre_gain, out_gain, gate_weight, up_weight, down_weight):
    row_count, col_part = hidden.shape
    tp_count = lax.axis_size("tp")
    req_count = lax.axis_size("req")
    full_width = col_part * tp_count
    copies = req_count // E
    slot_count = CAP // copies
    stream = hidden.astype(jnp.float32)
    whole_rows = lax.all_gather(hidden, "tp", axis=1, tiled=True).astype(jnp.float32)
    meansq = jnp.sum(whole_rows * whole_rows, axis=1) / full_width
    normed_in = (whole_rows * lax.rsqrt(meansq + epsilon)[:, None] * pre_gain[None, :]).astype(
        jnp.bfloat16
    )
    send_cols = normed_in.shape[1]
    top = routes.shape[1]
    chosen = routes.reshape(-1)
    onehot = (chosen[:, None] == jnp.arange(E, dtype=jnp.int32)[None, :]).astype(jnp.int32)
    slot_rank = jnp.sum((jnp.cumsum(onehot, axis=0) - 1) * onehot, axis=1)
    dest = (slot_rank % copies) * E + chosen
    out_idx = dest * slot_count + slot_rank // copies
    out_pairs = out_idx.reshape(row_count, top)
    slot_ids = jnp.arange(req_count * slot_count, dtype=jnp.int32)
    dispatch = jnp.zeros((req_count * slot_count, row_count), jnp.bool_)
    for k in range(top):
        dispatch = dispatch | (slot_ids[:, None] == out_pairs[None, :, k])
    outgoing = jnp.dot(
        dispatch.astype(jnp.bfloat16), normed_in, preferred_element_type=jnp.float32
    ).astype(jnp.bfloat16)
    outgoing = outgoing.reshape(req_count, slot_count, send_cols)
    pieces = lax.all_to_all(outgoing, "req", split_axis=0, concat_axis=0, tiled=True)
    sources, items, widths = pieces.shape
    flat_rows = pieces.reshape(sources * items, widths)
    gate_val = jnp.dot(flat_rows, gate_weight[0], preferred_element_type=jnp.float32)
    up_val = jnp.dot(flat_rows, up_weight[0], preferred_element_type=jnp.float32)
    activ = (jax.nn.silu(gate_val) * up_val).astype(jnp.bfloat16)
    partial_out = jnp.dot(activ, down_weight[0], preferred_element_type=jnp.float32)
    partial_out = lax.optimization_barrier(partial_out.astype(jnp.bfloat16)).astype(jnp.float32)
    summed = lax.psum_scatter(
        partial_out.reshape(sources, items, widths).astype(jnp.bfloat16),
        "tp",
        scatter_dimension=2,
        tiled=True,
    )
    returned = lax.all_to_all(summed, "req", split_axis=0, concat_axis=0, tiled=True)
    returned = returned.reshape(req_count * slot_count, col_part)
    picked = returned[out_idx].reshape(row_count, top, col_part).astype(jnp.float32)
    mixed = jnp.sum(picked * route_weights[:, :, None], axis=1)
    total_stream = stream + mixed
    out_sums = lax.psum(jnp.sum(total_stream * total_stream, axis=1), "tp")
    normed_out = (
        total_stream * lax.rsqrt(out_sums / full_width + epsilon)[:, None] * out_gain[None, :]
    )
    return (total_stream.astype(jnp.bfloat16), normed_out.astype(jnp.bfloat16))


def solution(mesh):
    return jax.shard_map(
        shards,
        mesh=mesh,
        in_specs=(
            P("req", "tp"),
            P("req", None),
            P("req", None),
            P(),
            P("tp"),
            P("req", None, "tp"),
            P("req", None, "tp"),
            P("req", "tp", None),
        ),
        out_specs=(P("req", "tp"), P("req", "tp")),
        check_vma=False,
    )
```

```python
import jax
import jax.numpy as jnp
from jax import lax
from jax.sharding import PartitionSpec as P

E = 8
CAP = 128
CHUNKS = 2


epsilon = 1e-05


def shards(hidden, routes, route_weights, pre_gain, out_gain, gate_weight, up_weight, down_weight):
    row_count, col_part = hidden.shape
    tp_count = lax.axis_size("tp")
    req_count = lax.axis_size("req")
    full_width = col_part * tp_count
    copies = req_count // E
    slot_count = CAP // copies
    chunk_items = slot_count // CHUNKS
    stream = hidden.astype(jnp.float32)
    whole_rows = lax.all_gather(hidden, "tp", axis=1, tiled=True).astype(jnp.float32)
    meansq = jnp.sum(whole_rows * whole_rows, axis=1) / full_width
    normed_in = (whole_rows * lax.rsqrt(meansq + epsilon)[:, None] * pre_gain[None, :]).astype(
        jnp.bfloat16
    )
    send_cols = normed_in.shape[1]
    top = routes.shape[1]
    chosen = routes.reshape(-1)
    onehot = (chosen[:, None] == jnp.arange(E, dtype=jnp.int32)[None, :]).astype(jnp.int32)
    slot_rank = jnp.sum((jnp.cumsum(onehot, axis=0) - 1) * onehot, axis=1)
    dest = (slot_rank % copies) * E + chosen
    item = slot_rank // copies
    chunk_of = item // chunk_items
    in_chunk = dest * chunk_items + item % chunk_items
    chunk_pairs = in_chunk.reshape(row_count, top)
    owner_pairs = chunk_of.reshape(row_count, top)
    slot_ids = jnp.arange(req_count * chunk_items, dtype=jnp.int32)
    returned = []
    for c in range(CHUNKS):
        dispatch = jnp.zeros((req_count * chunk_items, row_count), jnp.bool_)
        for k in range(top):
            hit = (slot_ids[:, None] == chunk_pairs[None, :, k]) & (owner_pairs[None, :, k] == c)
            dispatch = dispatch | hit
        outgoing = jnp.dot(
            dispatch.astype(jnp.bfloat16), normed_in, preferred_element_type=jnp.float32
        ).astype(jnp.bfloat16)
        outgoing = outgoing.reshape(req_count, chunk_items, send_cols)
        pieces = lax.all_to_all(outgoing, "req", split_axis=0, concat_axis=0, tiled=True)
        sources, items, widths = pieces.shape
        flat_rows = pieces.reshape(sources * items, widths)
        gate_val = jnp.dot(flat_rows, gate_weight[0], preferred_element_type=jnp.float32)
        up_val = jnp.dot(flat_rows, up_weight[0], preferred_element_type=jnp.float32)
        activ = (jax.nn.silu(gate_val) * up_val).astype(jnp.bfloat16)
        partial_out = jnp.dot(activ, down_weight[0], preferred_element_type=jnp.float32)
        partial_out = lax.optimization_barrier(partial_out.astype(jnp.bfloat16)).astype(jnp.float32)
        summed = lax.psum_scatter(
            partial_out.reshape(sources, items, widths).astype(jnp.bfloat16),
            "tp",
            scatter_dimension=2,
            tiled=True,
        )
        back = lax.all_to_all(summed, "req", split_axis=0, concat_axis=0, tiled=True)
        returned.append(back.reshape(req_count * chunk_items, col_part))
    returned = jnp.concatenate(returned, axis=0)
    out_idx = chunk_of * (req_count * chunk_items) + in_chunk
    picked = returned[out_idx].reshape(row_count, top, col_part).astype(jnp.float32)
    mixed = jnp.sum(picked * route_weights[:, :, None], axis=1)
    total_stream = stream + mixed
    out_sums = lax.psum(jnp.sum(total_stream * total_stream, axis=1), "tp")
    normed_out = (
        total_stream * lax.rsqrt(out_sums / full_width + epsilon)[:, None] * out_gain[None, :]
    )
    return (total_stream.astype(jnp.bfloat16), normed_out.astype(jnp.bfloat16))


def solution(mesh):
    return jax.shard_map(
        shards,
        mesh=mesh,
        in_specs=(
            P("req", "tp"),
            P("req", None),
            P("req", None),
            P(),
            P("tp"),
            P("req", None, "tp"),
            P("req", None, "tp"),
            P("req", "tp", None),
        ),
        out_specs=(P("req", "tp"), P("req", "tp")),
        check_vma=False,
    )
```

```python
import jax
import jax.numpy as jnp
from jax import lax
from jax.sharding import PartitionSpec as P

E = 8
CAP = 128
CHUNKS = 2


epsilon = 1e-05


def shift_tp(value, step, tp_count):
    return lax.ppermute(value, "tp", [(j, (j + step) % tp_count) for j in range(tp_count)])


def by_source(value, tp_count):
    me = lax.axis_index("tp")
    parts = [value] + [shift_tp(value, s, tp_count) for s in range(1, tp_count)]
    stacked = jnp.stack(parts)
    return jnp.take(stacked, (me - jnp.arange(tp_count)) % tp_count, axis=0)


def gather_tp(value, tp_count):
    rows, cols = value.shape
    ordered = by_source(value, tp_count)
    return ordered.transpose(1, 0, 2).reshape(rows, tp_count * cols)


def sum_tp(value, tp_count):
    ordered = by_source(value, tp_count)
    total = ordered[0]
    for s in range(1, tp_count):
        total = total + ordered[s]
    return total


def scatter_sum_tp(value, tp_count):
    me = lax.axis_index("tp")
    width = value.shape[1] // tp_count
    terms = []
    for s in range(tp_count):
        block = lax.dynamic_slice_in_dim(value, ((me + s) % tp_count) * width, width, axis=1)
        terms.append(block if s == 0 else shift_tp(block, s, tp_count))
    ordered = jnp.take(jnp.stack(terms), (me - jnp.arange(tp_count)) % tp_count, axis=0)
    total = ordered[0].astype(jnp.float32)
    for s in range(1, tp_count):
        total = total + ordered[s].astype(jnp.float32)
    return total.astype(value.dtype)


def shards(hidden, routes, route_weights, pre_gain, out_gain, gate_weight, up_weight, down_weight):
    row_count, col_part = hidden.shape
    tp_count = lax.axis_size("tp")
    req_count = lax.axis_size("req")
    full_width = col_part * tp_count
    copies = req_count // E
    slot_count = CAP // copies
    chunk_items = slot_count // CHUNKS
    stream = hidden.astype(jnp.float32)
    whole_rows = gather_tp(hidden, tp_count).astype(jnp.float32)
    meansq = jnp.sum(whole_rows * whole_rows, axis=1) / full_width
    normed_in = (whole_rows * lax.rsqrt(meansq + epsilon)[:, None] * pre_gain[None, :]).astype(
        jnp.bfloat16
    )
    send_cols = normed_in.shape[1]
    top = routes.shape[1]
    chosen = routes.reshape(-1)
    onehot = (chosen[:, None] == jnp.arange(E, dtype=jnp.int32)[None, :]).astype(jnp.int32)
    slot_rank = jnp.sum((jnp.cumsum(onehot, axis=0) - 1) * onehot, axis=1)
    dest = (slot_rank % copies) * E + chosen
    item = slot_rank // copies
    chunk_of = item // chunk_items
    in_chunk = dest * chunk_items + item % chunk_items
    chunk_pairs = in_chunk.reshape(row_count, top)
    owner_pairs = chunk_of.reshape(row_count, top)
    slot_ids = jnp.arange(req_count * chunk_items, dtype=jnp.int32)
    returned = []
    for c in range(CHUNKS):
        dispatch = jnp.zeros((req_count * chunk_items, row_count), jnp.bool_)
        for k in range(top):
            hit = (slot_ids[:, None] == chunk_pairs[None, :, k]) & (owner_pairs[None, :, k] == c)
            dispatch = dispatch | hit
        outgoing = jnp.dot(
            dispatch.astype(jnp.bfloat16), normed_in, preferred_element_type=jnp.float32
        ).astype(jnp.bfloat16)
        outgoing = outgoing.reshape(req_count, chunk_items, send_cols)
        pieces = lax.all_to_all(outgoing, "req", split_axis=0, concat_axis=0, tiled=True)
        sources, items, widths = pieces.shape
        flat_rows = pieces.reshape(sources * items, widths)
        gate_val = jnp.dot(flat_rows, gate_weight[0], preferred_element_type=jnp.float32)
        up_val = jnp.dot(flat_rows, up_weight[0], preferred_element_type=jnp.float32)
        activ = (jax.nn.silu(gate_val) * up_val).astype(jnp.bfloat16)
        partial_out = jnp.dot(activ, down_weight[0], preferred_element_type=jnp.float32)
        partial_out = lax.optimization_barrier(partial_out.astype(jnp.bfloat16)).astype(jnp.float32)
        summed = scatter_sum_tp(partial_out.astype(jnp.bfloat16), tp_count)
        summed = summed.reshape(sources, items, col_part)
        back = lax.all_to_all(summed, "req", split_axis=0, concat_axis=0, tiled=True)
        returned.append(back.reshape(req_count * chunk_items, col_part))
    returned = jnp.concatenate(returned, axis=0)
    out_idx = chunk_of * (req_count * chunk_items) + in_chunk
    picked = returned[out_idx].reshape(row_count, top, col_part).astype(jnp.float32)
    mixed = jnp.sum(picked * route_weights[:, :, None], axis=1)
    total_stream = stream + mixed
    out_sums = sum_tp(jnp.sum(total_stream * total_stream, axis=1), tp_count)
    normed_out = (
        total_stream * lax.rsqrt(out_sums / full_width + epsilon)[:, None] * out_gain[None, :]
    )
    return (total_stream.astype(jnp.bfloat16), normed_out.astype(jnp.bfloat16))


def solution(mesh):
    return jax.shard_map(
        shards,
        mesh=mesh,
        in_specs=(
            P("req", "tp"),
            P("req", None),
            P("req", None),
            P(),
            P("tp"),
            P("req", None, "tp"),
            P("req", None, "tp"),
            P("req", "tp", None),
        ),
        out_specs=(P("req", "tp"), P("req", "tp")),
        check_vma=False,
    )
```

```python
import jax
import jax.numpy as jnp
from jax import lax
from jax.sharding import PartitionSpec as P

E = 8
CAP = 128
CHUNKS = 2


epsilon = 1e-05


def shift_tp(value, step, tp_count):
    return lax.ppermute(value, "tp", [(j, (j + step) % tp_count) for j in range(tp_count)])


def by_source(value, tp_count):
    me = lax.axis_index("tp")
    parts = [value] + [shift_tp(value, s, tp_count) for s in range(1, tp_count)]
    stacked = jnp.stack(parts)
    return jnp.take(stacked, (me - jnp.arange(tp_count)) % tp_count, axis=0)


def gather_tp(value, tp_count):
    me = lax.axis_index("tp")
    rows, cols = value.shape
    whole = jnp.zeros((rows, tp_count * cols), value.dtype)
    for s in range(tp_count):
        part = value if s == 0 else shift_tp(value, s, tp_count)
        whole = lax.dynamic_update_slice_in_dim(whole, part, ((me - s) % tp_count) * cols, axis=1)
    return whole


def sum_tp(value, tp_count):
    ordered = by_source(value, tp_count)
    total = ordered[0]
    for s in range(1, tp_count):
        total = total + ordered[s]
    return total


def scatter_sum_tp(value, tp_count):
    me = lax.axis_index("tp")
    width = value.shape[1] // tp_count
    terms = []
    for s in range(tp_count):
        block = lax.dynamic_slice_in_dim(value, ((me + s) % tp_count) * width, width, axis=1)
        terms.append(block if s == 0 else shift_tp(block, s, tp_count))
    total = terms[0].astype(jnp.float32)
    for s in range(1, tp_count):
        total = total + terms[s].astype(jnp.float32)
    return total.astype(value.dtype)


def shards(hidden, routes, route_weights, pre_gain, out_gain, gate_weight, up_weight, down_weight):
    row_count, col_part = hidden.shape
    tp_count = lax.axis_size("tp")
    req_count = lax.axis_size("req")
    full_width = col_part * tp_count
    copies = req_count // E
    slot_count = CAP // copies
    chunk_items = slot_count // CHUNKS
    stream = hidden.astype(jnp.float32)
    whole_rows = gather_tp(hidden, tp_count).astype(jnp.float32)
    meansq = jnp.sum(whole_rows * whole_rows, axis=1) / full_width
    normed_in = (whole_rows * lax.rsqrt(meansq + epsilon)[:, None] * pre_gain[None, :]).astype(
        jnp.bfloat16
    )
    send_cols = normed_in.shape[1]
    top = routes.shape[1]
    chosen = routes.reshape(-1)
    onehot = (chosen[:, None] == jnp.arange(E, dtype=jnp.int32)[None, :]).astype(jnp.int32)
    slot_rank = jnp.sum((jnp.cumsum(onehot, axis=0) - 1) * onehot, axis=1)
    dest = (slot_rank % copies) * E + chosen
    item = slot_rank // copies
    chunk_of = item // chunk_items
    in_chunk = dest * chunk_items + item % chunk_items
    chunk_pairs = in_chunk.reshape(row_count, top)
    owner_pairs = chunk_of.reshape(row_count, top)
    slot_ids = jnp.arange(req_count * chunk_items, dtype=jnp.int32)
    returned = []
    for c in range(CHUNKS):
        dispatch = jnp.zeros((req_count * chunk_items, row_count), jnp.bool_)
        for k in range(top):
            hit = (slot_ids[:, None] == chunk_pairs[None, :, k]) & (owner_pairs[None, :, k] == c)
            dispatch = dispatch | hit
        outgoing = jnp.dot(
            dispatch.astype(jnp.bfloat16), normed_in, preferred_element_type=jnp.float32
        ).astype(jnp.bfloat16)
        outgoing = outgoing.reshape(req_count, chunk_items, send_cols)
        pieces = lax.all_to_all(outgoing, "req", split_axis=0, concat_axis=0, tiled=True)
        sources, items, widths = pieces.shape
        flat_rows = pieces.reshape(sources * items, widths)
        gate_val = jnp.dot(flat_rows, gate_weight[0], preferred_element_type=jnp.float32)
        up_val = jnp.dot(flat_rows, up_weight[0], preferred_element_type=jnp.float32)
        activ = (jax.nn.silu(gate_val) * up_val).astype(jnp.bfloat16)
        partial_out = jnp.dot(activ, down_weight[0], preferred_element_type=jnp.float32)
        partial_out = lax.optimization_barrier(partial_out.astype(jnp.bfloat16)).astype(jnp.float32)
        summed = scatter_sum_tp(partial_out.astype(jnp.bfloat16), tp_count)
        summed = summed.reshape(sources, items, col_part)
        back = lax.all_to_all(summed, "req", split_axis=0, concat_axis=0, tiled=True)
        returned.append(back.reshape(req_count * chunk_items, col_part))
    returned = jnp.concatenate(returned, axis=0)
    out_idx = chunk_of * (req_count * chunk_items) + in_chunk
    picked = returned[out_idx].reshape(row_count, top, col_part).astype(jnp.float32)
    mixed = jnp.sum(picked * route_weights[:, :, None], axis=1)
    total_stream = stream + mixed
    out_sums = sum_tp(jnp.sum(total_stream * total_stream, axis=1), tp_count)
    normed_out = (
        total_stream * lax.rsqrt(out_sums / full_width + epsilon)[:, None] * out_gain[None, :]
    )
    return (total_stream.astype(jnp.bfloat16), normed_out.astype(jnp.bfloat16))


def solution(mesh):
    return jax.shard_map(
        shards,
        mesh=mesh,
        in_specs=(
            P("req", "tp"),
            P("req", None),
            P("req", None),
            P(),
            P("tp"),
            P("req", None, "tp"),
            P("req", None, "tp"),
            P("req", "tp", None),
        ),
        out_specs=(P("req", "tp"), P("req", "tp")),
        check_vma=False,
    )
```

```python
import jax
import jax.numpy as jnp
from jax import lax
from jax.sharding import PartitionSpec as P

E = 8
CAP = 128
CHUNKS = 4


epsilon = 1e-05


def shift_tp(value, step, tp_count):
    return lax.ppermute(value, "tp", [(j, (j + step) % tp_count) for j in range(tp_count)])


def by_source(value, tp_count):
    me = lax.axis_index("tp")
    parts = [value] + [shift_tp(value, s, tp_count) for s in range(1, tp_count)]
    stacked = jnp.stack(parts)
    return jnp.take(stacked, (me - jnp.arange(tp_count)) % tp_count, axis=0)


def gather_tp(value, tp_count):
    me = lax.axis_index("tp")
    rows, cols = value.shape
    whole = jnp.zeros((rows, tp_count * cols), value.dtype)
    for s in range(tp_count):
        part = value if s == 0 else shift_tp(value, s, tp_count)
        whole = lax.dynamic_update_slice_in_dim(whole, part, ((me - s) % tp_count) * cols, axis=1)
    return whole


def sum_tp(value, tp_count):
    ordered = by_source(value, tp_count)
    total = ordered[0]
    for s in range(1, tp_count):
        total = total + ordered[s]
    return total


def scatter_sum_tp(value, tp_count):
    me = lax.axis_index("tp")
    width = value.shape[1] // tp_count
    terms = []
    for s in range(tp_count):
        block = lax.dynamic_slice_in_dim(value, ((me + s) % tp_count) * width, width, axis=1)
        terms.append(block if s == 0 else shift_tp(block, s, tp_count))
    total = terms[0].astype(jnp.float32)
    for s in range(1, tp_count):
        total = total + terms[s].astype(jnp.float32)
    return total.astype(value.dtype)


def shards(hidden, routes, route_weights, pre_gain, out_gain, gate_weight, up_weight, down_weight):
    row_count, col_part = hidden.shape
    tp_count = lax.axis_size("tp")
    req_count = lax.axis_size("req")
    full_width = col_part * tp_count
    copies = req_count // E
    slot_count = CAP // copies
    chunk_items = slot_count // CHUNKS
    stream = hidden.astype(jnp.float32)
    whole_rows = gather_tp(hidden, tp_count).astype(jnp.float32)
    meansq = jnp.sum(whole_rows * whole_rows, axis=1) / full_width
    normed_in = (whole_rows * lax.rsqrt(meansq + epsilon)[:, None] * pre_gain[None, :]).astype(
        jnp.bfloat16
    )
    send_cols = normed_in.shape[1]
    top = routes.shape[1]
    chosen = routes.reshape(-1)
    onehot = (chosen[:, None] == jnp.arange(E, dtype=jnp.int32)[None, :]).astype(jnp.int32)
    slot_rank = jnp.sum((jnp.cumsum(onehot, axis=0) - 1) * onehot, axis=1)
    dest = (slot_rank % copies) * E + chosen
    item = slot_rank // copies
    chunk_of = item // chunk_items
    in_chunk = dest * chunk_items + item % chunk_items
    chunk_pairs = in_chunk.reshape(row_count, top)
    owner_pairs = chunk_of.reshape(row_count, top)
    slot_ids = jnp.arange(req_count * chunk_items, dtype=jnp.int32)
    returned = []
    for c in range(CHUNKS):
        dispatch = jnp.zeros((req_count * chunk_items, row_count), jnp.bool_)
        for k in range(top):
            hit = (slot_ids[:, None] == chunk_pairs[None, :, k]) & (owner_pairs[None, :, k] == c)
            dispatch = dispatch | hit
        outgoing = jnp.dot(
            dispatch.astype(jnp.bfloat16), normed_in, preferred_element_type=jnp.float32
        ).astype(jnp.bfloat16)
        outgoing = outgoing.reshape(req_count, chunk_items, send_cols)
        pieces = lax.all_to_all(outgoing, "req", split_axis=0, concat_axis=0, tiled=True)
        sources, items, widths = pieces.shape
        flat_rows = pieces.reshape(sources * items, widths)
        gate_val = jnp.dot(flat_rows, gate_weight[0], preferred_element_type=jnp.float32)
        up_val = jnp.dot(flat_rows, up_weight[0], preferred_element_type=jnp.float32)
        activ = (jax.nn.silu(gate_val) * up_val).astype(jnp.bfloat16)
        partial_out = jnp.dot(activ, down_weight[0], preferred_element_type=jnp.float32)
        partial_out = lax.optimization_barrier(partial_out.astype(jnp.bfloat16)).astype(jnp.float32)
        summed = scatter_sum_tp(partial_out.astype(jnp.bfloat16), tp_count)
        summed = summed.reshape(sources, items, col_part)
        back = lax.all_to_all(summed, "req", split_axis=0, concat_axis=0, tiled=True)
        returned.append(back.reshape(req_count * chunk_items, col_part))
    returned = jnp.concatenate(returned, axis=0)
    out_idx = chunk_of * (req_count * chunk_items) + in_chunk
    picked = returned[out_idx].reshape(row_count, top, col_part).astype(jnp.float32)
    mixed = jnp.sum(picked * route_weights[:, :, None], axis=1)
    total_stream = stream + mixed
    out_sums = sum_tp(jnp.sum(total_stream * total_stream, axis=1), tp_count)
    normed_out = (
        total_stream * lax.rsqrt(out_sums / full_width + epsilon)[:, None] * out_gain[None, :]
    )
    return (total_stream.astype(jnp.bfloat16), normed_out.astype(jnp.bfloat16))


def solution(mesh):
    return jax.shard_map(
        shards,
        mesh=mesh,
        in_specs=(
            P("req", "tp"),
            P("req", None),
            P("req", None),
            P(),
            P("tp"),
            P("req", None, "tp"),
            P("req", None, "tp"),
            P("req", "tp", None),
        ),
        out_specs=(P("req", "tp"), P("req", "tp")),
        check_vma=False,
    )
```

```python
import jax
import jax.numpy as jnp
from jax import lax
from jax.sharding import PartitionSpec as P

E = 8
CAP = 128
CHUNKS = 2


epsilon = 1e-05


def shift_tp(value, step, tp_count):
    return lax.ppermute(value, "tp", [(j, (j + step) % tp_count) for j in range(tp_count)])


def by_source(value, tp_count):
    me = lax.axis_index("tp")
    parts = [value] + [shift_tp(value, s, tp_count) for s in range(1, tp_count)]
    stacked = jnp.stack(parts)
    return jnp.take(stacked, (me - jnp.arange(tp_count)) % tp_count, axis=0)


def gather_tp(value, tp_count):
    me = lax.axis_index("tp")
    rows, cols = value.shape
    whole = jnp.zeros((rows, tp_count * cols), value.dtype)
    for s in range(tp_count):
        part = value if s == 0 else shift_tp(value, s, tp_count)
        whole = lax.dynamic_update_slice_in_dim(whole, part, ((me - s) % tp_count) * cols, axis=1)
    return whole


def sum_tp(value, tp_count):
    ordered = by_source(value, tp_count)
    total = ordered[0]
    for s in range(1, tp_count):
        total = total + ordered[s]
    return total


def down_scatter_sum_tp(activ, w_down, tp_count):
    me = lax.axis_index("tp")
    width = w_down.shape[1] // tp_count
    terms = []
    for s in list(range(1, tp_count)) + [0]:
        w_block = lax.dynamic_slice_in_dim(w_down, ((me + s) % tp_count) * width, width, axis=1)
        block = jnp.dot(activ, w_block, preferred_element_type=jnp.float32).astype(jnp.bfloat16)
        terms.append(block if s == 0 else shift_tp(block, s, tp_count))
    total = terms[0].astype(jnp.float32)
    for term in terms[1:]:
        total = total + term.astype(jnp.float32)
    return total.astype(jnp.bfloat16)


def shards(hidden, routes, route_weights, pre_gain, out_gain, gate_weight, up_weight, down_weight):
    row_count, col_part = hidden.shape
    tp_count = lax.axis_size("tp")
    req_count = lax.axis_size("req")
    full_width = col_part * tp_count
    copies = req_count // E
    slot_count = CAP // copies
    chunk_items = slot_count // CHUNKS
    stream = hidden.astype(jnp.float32)
    whole_rows = gather_tp(hidden, tp_count).astype(jnp.float32)
    meansq = jnp.sum(whole_rows * whole_rows, axis=1) / full_width
    normed_in = (whole_rows * lax.rsqrt(meansq + epsilon)[:, None] * pre_gain[None, :]).astype(
        jnp.bfloat16
    )
    send_cols = normed_in.shape[1]
    top = routes.shape[1]
    chosen = routes.reshape(-1)
    onehot = (chosen[:, None] == jnp.arange(E, dtype=jnp.int32)[None, :]).astype(jnp.int32)
    slot_rank = jnp.sum((jnp.cumsum(onehot, axis=0) - 1) * onehot, axis=1)
    dest = (slot_rank % copies) * E + chosen
    item = slot_rank // copies
    chunk_of = item // chunk_items
    in_chunk = dest * chunk_items + item % chunk_items
    chunk_pairs = in_chunk.reshape(row_count, top)
    owner_pairs = chunk_of.reshape(row_count, top)
    slot_ids = jnp.arange(req_count * chunk_items, dtype=jnp.int32)
    returned = []
    for c in range(CHUNKS):
        dispatch = jnp.zeros((req_count * chunk_items, row_count), jnp.bool_)
        for k in range(top):
            hit = (slot_ids[:, None] == chunk_pairs[None, :, k]) & (owner_pairs[None, :, k] == c)
            dispatch = dispatch | hit
        outgoing = jnp.dot(
            dispatch.astype(jnp.bfloat16), normed_in, preferred_element_type=jnp.float32
        ).astype(jnp.bfloat16)
        outgoing = outgoing.reshape(req_count, chunk_items, send_cols)
        pieces = lax.all_to_all(outgoing, "req", split_axis=0, concat_axis=0, tiled=True)
        sources, items, widths = pieces.shape
        flat_rows = pieces.reshape(sources * items, widths)
        gate_val = jnp.dot(flat_rows, gate_weight[0], preferred_element_type=jnp.float32)
        up_val = jnp.dot(flat_rows, up_weight[0], preferred_element_type=jnp.float32)
        activ = (jax.nn.silu(gate_val) * up_val).astype(jnp.bfloat16)
        summed = down_scatter_sum_tp(activ, down_weight[0], tp_count)
        summed = summed.reshape(sources, items, col_part)
        back = lax.all_to_all(summed, "req", split_axis=0, concat_axis=0, tiled=True)
        returned.append(back.reshape(req_count * chunk_items, col_part))
    returned = jnp.concatenate(returned, axis=0)
    out_idx = chunk_of * (req_count * chunk_items) + in_chunk
    picked = returned[out_idx].reshape(row_count, top, col_part).astype(jnp.float32)
    mixed = jnp.sum(picked * route_weights[:, :, None], axis=1)
    total_stream = stream + mixed
    out_sums = sum_tp(jnp.sum(total_stream * total_stream, axis=1), tp_count)
    normed_out = (
        total_stream * lax.rsqrt(out_sums / full_width + epsilon)[:, None] * out_gain[None, :]
    )
    return (total_stream.astype(jnp.bfloat16), normed_out.astype(jnp.bfloat16))


def solution(mesh):
    return jax.shard_map(
        shards,
        mesh=mesh,
        in_specs=(
            P("req", "tp"),
            P("req", None),
            P("req", None),
            P(),
            P("tp"),
            P("req", None, "tp"),
            P("req", None, "tp"),
            P("req", "tp", None),
        ),
        out_specs=(P("req", "tp"), P("req", "tp")),
        check_vma=False,
    )
```

```python
import jax
import jax.numpy as jnp
from jax import lax
from jax.sharding import PartitionSpec as P

E = 8
CAP = 128
CHUNKS = 2


epsilon = 1e-05


def shift_tp(value, step, tp_count):
    return lax.ppermute(value, "tp", [(j, (j + step) % tp_count) for j in range(tp_count)])


def by_source(value, tp_count):
    me = lax.axis_index("tp")
    parts = [value] + [shift_tp(value, s, tp_count) for s in range(1, tp_count)]
    stacked = jnp.stack(parts)
    return jnp.take(stacked, (me - jnp.arange(tp_count)) % tp_count, axis=0)


def gather_tp(value, tp_count):
    me = lax.axis_index("tp")
    rows, cols = value.shape
    whole = jnp.zeros((rows, tp_count * cols), value.dtype)
    for s in range(tp_count):
        part = value if s == 0 else shift_tp(value, s, tp_count)
        whole = lax.dynamic_update_slice_in_dim(whole, part, ((me - s) % tp_count) * cols, axis=1)
    return whole


def sum_tp(value, tp_count):
    ordered = by_source(value, tp_count)
    total = ordered[0]
    for s in range(1, tp_count):
        total = total + ordered[s]
    return total


def down_scatter_sum_tp(activ, w_down, tp_count):
    me = lax.axis_index("tp")
    width = w_down.shape[1] // tp_count
    terms = []
    for s in list(range(1, tp_count)) + [0]:
        w_block = lax.dynamic_slice_in_dim(w_down, ((me + s) % tp_count) * width, width, axis=1)
        block = jnp.dot(activ, w_block, preferred_element_type=jnp.float32).astype(jnp.bfloat16)
        terms.append(block if s == 0 else shift_tp(block, s, tp_count))
    total = terms[0].astype(jnp.float32)
    for term in terms[1:]:
        total = total + term.astype(jnp.float32)
    return total.astype(jnp.bfloat16)


def shards(hidden, routes, route_weights, pre_gain, out_gain, gate_weight, up_weight, down_weight):
    row_count, col_part = hidden.shape
    tp_count = lax.axis_size("tp")
    req_count = lax.axis_size("req")
    full_width = col_part * tp_count
    copies = req_count // E
    slot_count = CAP // copies
    chunk_items = slot_count // CHUNKS
    stream = hidden.astype(jnp.float32)
    whole_rows = gather_tp(hidden, tp_count).astype(jnp.float32)
    meansq = sum_tp(jnp.sum(stream * stream, axis=1), tp_count) / full_width
    row_scale = lax.rsqrt(meansq + epsilon)[:, None]
    normed_in = (whole_rows * row_scale * pre_gain[None, :]).astype(jnp.bfloat16)
    own_gain = lax.dynamic_slice_in_dim(pre_gain, lax.axis_index("tp") * col_part, col_part)
    normed_own = (stream * row_scale * own_gain[None, :]).astype(jnp.bfloat16)
    top = routes.shape[1]
    chosen = routes.reshape(-1)
    onehot = (chosen[:, None] == jnp.arange(E, dtype=jnp.int32)[None, :]).astype(jnp.int32)
    slot_rank = jnp.sum((jnp.cumsum(onehot, axis=0) - 1) * onehot, axis=1)
    dest = (slot_rank % copies) * E + chosen
    item = slot_rank // copies
    chunk_of = item // chunk_items
    in_chunk = dest * chunk_items + item % chunk_items
    chunk_pairs = in_chunk.reshape(row_count, top)
    owner_pairs = chunk_of.reshape(row_count, top)
    slot_ids = jnp.arange(req_count * chunk_items, dtype=jnp.int32)
    returned = []
    for c in range(CHUNKS):
        dispatch = jnp.zeros((req_count * chunk_items, row_count), jnp.bool_)
        for k in range(top):
            hit = (slot_ids[:, None] == chunk_pairs[None, :, k]) & (owner_pairs[None, :, k] == c)
            dispatch = dispatch | hit
        relay = c == 0
        source = normed_own if relay else normed_in
        outgoing = jnp.dot(
            dispatch.astype(jnp.bfloat16), source, preferred_element_type=jnp.float32
        ).astype(jnp.bfloat16)
        outgoing = outgoing.reshape(req_count, chunk_items, source.shape[1])
        pieces = lax.all_to_all(outgoing, "req", split_axis=0, concat_axis=0, tiled=True)
        sources, items, widths = pieces.shape
        flat_rows = pieces.reshape(sources * items, widths)
        if relay:
            flat_rows = gather_tp(flat_rows, tp_count)
        gate_val = jnp.dot(flat_rows, gate_weight[0], preferred_element_type=jnp.float32)
        up_val = jnp.dot(flat_rows, up_weight[0], preferred_element_type=jnp.float32)
        activ = (jax.nn.silu(gate_val) * up_val).astype(jnp.bfloat16)
        summed = down_scatter_sum_tp(activ, down_weight[0], tp_count)
        summed = summed.reshape(sources, items, col_part)
        back = lax.all_to_all(summed, "req", split_axis=0, concat_axis=0, tiled=True)
        returned.append(back.reshape(req_count * chunk_items, col_part))
    returned = jnp.concatenate(returned, axis=0)
    out_idx = chunk_of * (req_count * chunk_items) + in_chunk
    picked = returned[out_idx].reshape(row_count, top, col_part).astype(jnp.float32)
    mixed = jnp.sum(picked * route_weights[:, :, None], axis=1)
    total_stream = stream + mixed
    out_sums = sum_tp(jnp.sum(total_stream * total_stream, axis=1), tp_count)
    normed_out = (
        total_stream * lax.rsqrt(out_sums / full_width + epsilon)[:, None] * out_gain[None, :]
    )
    return (total_stream.astype(jnp.bfloat16), normed_out.astype(jnp.bfloat16))


def solution(mesh):
    return jax.shard_map(
        shards,
        mesh=mesh,
        in_specs=(
            P("req", "tp"),
            P("req", None),
            P("req", None),
            P(),
            P("tp"),
            P("req", None, "tp"),
            P("req", None, "tp"),
            P("req", "tp", None),
        ),
        out_specs=(P("req", "tp"), P("req", "tp")),
        check_vma=False,
    )
```

```python
import jax
import jax.numpy as jnp
from jax import lax
from jax.sharding import PartitionSpec as P

E = 8
CAP = 128
CHUNKS = 2


epsilon = 1e-05


def rms_norm(values, gain):
    meansq = jnp.mean(values * values, axis=1, keepdims=True)
    return values * lax.rsqrt(meansq + epsilon) * gain[None, :]


def shift_tp(value, step, tp_count):
    return lax.ppermute(value, "tp", [(j, (j + step) % tp_count) for j in range(tp_count)])


def by_source(value, tp_count):
    me = lax.axis_index("tp")
    parts = [value] + [shift_tp(value, s, tp_count) for s in range(1, tp_count)]
    stacked = jnp.stack(parts)
    return jnp.take(stacked, (me - jnp.arange(tp_count)) % tp_count, axis=0)


def gather_tp(value, tp_count):
    me = lax.axis_index("tp")
    rows, cols = value.shape
    whole = jnp.zeros((rows, tp_count * cols), value.dtype)
    for s in range(tp_count):
        part = value if s == 0 else shift_tp(value, s, tp_count)
        whole = lax.dynamic_update_slice_in_dim(whole, part, ((me - s) % tp_count) * cols, axis=1)
    return whole


def sum_tp(value, tp_count):
    ordered = by_source(value, tp_count)
    total = ordered[0]
    for s in range(1, tp_count):
        total = total + ordered[s]
    return total


def down_scatter_sum_tp(activ, w_down, tp_count):
    me = lax.axis_index("tp")
    width = w_down.shape[1] // tp_count
    terms = []
    for s in list(range(1, tp_count)) + [0]:
        w_block = lax.dynamic_slice_in_dim(w_down, ((me + s) % tp_count) * width, width, axis=1)
        block = jnp.dot(activ, w_block, preferred_element_type=jnp.float32).astype(jnp.bfloat16)
        terms.append(block if s == 0 else shift_tp(block, s, tp_count))
    total = terms[0].astype(jnp.float32)
    for term in terms[1:]:
        total = total + term.astype(jnp.float32)
    return total.astype(jnp.bfloat16)


def shards(hidden, routes, route_weights, pre_gain, out_gain, gate_weight, up_weight, down_weight):
    row_count, col_part = hidden.shape
    tp_count = lax.axis_size("tp")
    req_count = lax.axis_size("req")
    full_width = col_part * tp_count
    copies = req_count // E
    slot_count = CAP // copies
    chunk_items = slot_count // CHUNKS
    stream = hidden.astype(jnp.float32)
    whole_rows = gather_tp(hidden, tp_count).astype(jnp.float32)
    normed_in = rms_norm(whole_rows, pre_gain).astype(jnp.bfloat16)
    top = routes.shape[1]
    chosen = routes.reshape(-1)
    onehot = (chosen[:, None] == jnp.arange(E, dtype=jnp.int32)[None, :]).astype(jnp.int32)
    slot_rank = jnp.sum((jnp.cumsum(onehot, axis=0) - 1) * onehot, axis=1)
    dest = (slot_rank % copies) * E + chosen
    item = slot_rank // copies
    chunk_of = item // chunk_items
    in_chunk = dest * chunk_items + item % chunk_items
    chunk_pairs = in_chunk.reshape(row_count, top)
    owner_pairs = chunk_of.reshape(row_count, top)
    slot_ids = jnp.arange(req_count * chunk_items, dtype=jnp.int32)
    returned = []
    for c in range(CHUNKS):
        dispatch = jnp.zeros((req_count * chunk_items, row_count), jnp.bool_)
        for k in range(top):
            hit = (slot_ids[:, None] == chunk_pairs[None, :, k]) & (owner_pairs[None, :, k] == c)
            dispatch = dispatch | hit
        relay = c == 0
        source = hidden if relay else normed_in
        outgoing = jnp.dot(
            dispatch.astype(jnp.bfloat16), source, preferred_element_type=jnp.float32
        ).astype(jnp.bfloat16)
        outgoing = outgoing.reshape(req_count, chunk_items, source.shape[1])
        pieces = lax.all_to_all(outgoing, "req", split_axis=0, concat_axis=0, tiled=True)
        sources, items, widths = pieces.shape
        flat_rows = pieces.reshape(sources * items, widths)
        if relay:
            raw_rows = gather_tp(flat_rows, tp_count).astype(jnp.float32)
            flat_rows = rms_norm(raw_rows, pre_gain).astype(jnp.bfloat16)
        gate_val = jnp.dot(flat_rows, gate_weight[0], preferred_element_type=jnp.float32)
        up_val = jnp.dot(flat_rows, up_weight[0], preferred_element_type=jnp.float32)
        activ = (jax.nn.silu(gate_val) * up_val).astype(jnp.bfloat16)
        summed = down_scatter_sum_tp(activ, down_weight[0], tp_count)
        summed = summed.reshape(sources, items, col_part)
        back = lax.all_to_all(summed, "req", split_axis=0, concat_axis=0, tiled=True)
        returned.append(back.reshape(req_count * chunk_items, col_part))
    total_stream = stream
    for c in range(CHUNKS):
        picked = returned[c][in_chunk].reshape(row_count, top, col_part).astype(jnp.float32)
        mine = (owner_pairs == c)[:, :, None]
        terms = jnp.where(mine, picked * route_weights[:, :, None], 0.0)
        total_stream = total_stream + jnp.sum(terms, axis=1)
    out_sums = sum_tp(jnp.sum(total_stream * total_stream, axis=1), tp_count)
    normed_out = (
        total_stream * lax.rsqrt(out_sums / full_width + epsilon)[:, None] * out_gain[None, :]
    )
    return (total_stream.astype(jnp.bfloat16), normed_out.astype(jnp.bfloat16))


def solution(mesh):
    return jax.shard_map(
        shards,
        mesh=mesh,
        in_specs=(
            P("req", "tp"),
            P("req", None),
            P("req", None),
            P(),
            P("tp"),
            P("req", None, "tp"),
            P("req", None, "tp"),
            P("req", "tp", None),
        ),
        out_specs=(P("req", "tp"), P("req", "tp")),
        check_vma=False,
    )
```

```python
import jax
import jax.numpy as jnp
from jax import lax
from jax.sharding import PartitionSpec as P

E = 8
CAP = 128
CHUNKS = 2


epsilon = 1e-05


def rms_norm(values, gain):
    meansq = jnp.mean(values * values, axis=1, keepdims=True)
    return values * lax.rsqrt(meansq + epsilon) * gain[None, :]


def shift_tp(value, step, tp_count):
    return lax.ppermute(value, "tp", [(j, (j + step) % tp_count) for j in range(tp_count)])


def by_source(value, tp_count):
    me = lax.axis_index("tp")
    parts = [value] + [shift_tp(value, s, tp_count) for s in range(1, tp_count)]
    stacked = jnp.stack(parts)
    return jnp.take(stacked, (me - jnp.arange(tp_count)) % tp_count, axis=0)


def exchange_tp(blocks, tp_count):
    if tp_count != 4:
        return [None] + [shift_tp(blocks[s], s, tp_count) for s in range(1, tp_count)]
    half = blocks[2].shape[0] // 2
    rows = blocks[1].shape[0]
    up = shift_tp(jnp.concatenate([blocks[1], blocks[2][:half]], axis=0), 1, tp_count)
    down = shift_tp(jnp.concatenate([blocks[3], blocks[2][half:]], axis=0), 3, tp_count)
    far_up = shift_tp(up[rows:], 1, tp_count)
    far_down = shift_tp(down[rows:], 3, tp_count)
    return [None, up[:rows], jnp.concatenate([far_up, far_down], axis=0), down[:rows]]


def gather_tp(value, tp_count):
    me = lax.axis_index("tp")
    rows, cols = value.shape
    came = exchange_tp([None] + [value] * (tp_count - 1), tp_count)
    whole = jnp.zeros((rows, tp_count * cols), value.dtype)
    for s in range(tp_count):
        part = value if s == 0 else came[s]
        whole = lax.dynamic_update_slice_in_dim(whole, part, ((me - s) % tp_count) * cols, axis=1)
    return whole


def sum_tp(value, tp_count):
    ordered = by_source(value, tp_count)
    total = ordered[0]
    for s in range(1, tp_count):
        total = total + ordered[s]
    return total


def down_scatter_sum_tp(activ, w_down, tp_count):
    me = lax.axis_index("tp")
    width = w_down.shape[1] // tp_count
    blocks = {}
    for s in list(range(tp_count - 1, 0, -1)) + [0]:
        w_block = lax.dynamic_slice_in_dim(w_down, ((me + s) % tp_count) * width, width, axis=1)
        blocks[s] = jnp.dot(activ, w_block, preferred_element_type=jnp.float32).astype(jnp.bfloat16)
    came = exchange_tp([blocks[s] for s in range(tp_count)], tp_count)
    total = blocks[0].astype(jnp.float32)
    for term in came[1:]:
        total = total + term.astype(jnp.float32)
    return total.astype(jnp.bfloat16)


def shards(hidden, routes, route_weights, pre_gain, out_gain, gate_weight, up_weight, down_weight):
    row_count, col_part = hidden.shape
    tp_count = lax.axis_size("tp")
    req_count = lax.axis_size("req")
    full_width = col_part * tp_count
    copies = req_count // E
    slot_count = CAP // copies
    chunk_items = slot_count // CHUNKS
    stream = hidden.astype(jnp.float32)
    whole_rows = gather_tp(hidden, tp_count).astype(jnp.float32)
    normed_in = rms_norm(whole_rows, pre_gain).astype(jnp.bfloat16)
    top = routes.shape[1]
    chosen = routes.reshape(-1)
    onehot = (chosen[:, None] == jnp.arange(E, dtype=jnp.int32)[None, :]).astype(jnp.int32)
    slot_rank = jnp.sum((jnp.cumsum(onehot, axis=0) - 1) * onehot, axis=1)
    dest = (slot_rank % copies) * E + chosen
    item = slot_rank // copies
    chunk_of = item // chunk_items
    in_chunk = dest * chunk_items + item % chunk_items
    chunk_pairs = in_chunk.reshape(row_count, top)
    owner_pairs = chunk_of.reshape(row_count, top)
    slot_ids = jnp.arange(req_count * chunk_items, dtype=jnp.int32)
    returned = []
    for c in range(CHUNKS):
        dispatch = jnp.zeros((req_count * chunk_items, row_count), jnp.bool_)
        for k in range(top):
            hit = (slot_ids[:, None] == chunk_pairs[None, :, k]) & (owner_pairs[None, :, k] == c)
            dispatch = dispatch | hit
        relay = c == 0
        source = hidden if relay else normed_in
        outgoing = jnp.dot(
            dispatch.astype(jnp.bfloat16), source, preferred_element_type=jnp.float32
        ).astype(jnp.bfloat16)
        outgoing = outgoing.reshape(req_count, chunk_items, source.shape[1])
        pieces = lax.all_to_all(outgoing, "req", split_axis=0, concat_axis=0, tiled=True)
        sources, items, widths = pieces.shape
        flat_rows = pieces.reshape(sources * items, widths)
        if relay:
            raw_rows = gather_tp(flat_rows, tp_count).astype(jnp.float32)
            flat_rows = rms_norm(raw_rows, pre_gain).astype(jnp.bfloat16)
        gate_val = jnp.dot(flat_rows, gate_weight[0], preferred_element_type=jnp.float32)
        up_val = jnp.dot(flat_rows, up_weight[0], preferred_element_type=jnp.float32)
        activ = (jax.nn.silu(gate_val) * up_val).astype(jnp.bfloat16)
        summed = down_scatter_sum_tp(activ, down_weight[0], tp_count)
        summed = summed.reshape(sources, items, col_part)
        back = lax.all_to_all(summed, "req", split_axis=0, concat_axis=0, tiled=True)
        returned.append(back.reshape(req_count * chunk_items, col_part))
    total_stream = stream
    for c in range(CHUNKS):
        picked = returned[c][in_chunk].reshape(row_count, top, col_part).astype(jnp.float32)
        mine = (owner_pairs == c)[:, :, None]
        terms = jnp.where(mine, picked * route_weights[:, :, None], 0.0)
        total_stream = total_stream + jnp.sum(terms, axis=1)
    out_sums = sum_tp(jnp.sum(total_stream * total_stream, axis=1), tp_count)
    normed_out = (
        total_stream * lax.rsqrt(out_sums / full_width + epsilon)[:, None] * out_gain[None, :]
    )
    return (total_stream.astype(jnp.bfloat16), normed_out.astype(jnp.bfloat16))


def solution(mesh):
    return jax.shard_map(
        shards,
        mesh=mesh,
        in_specs=(
            P("req", "tp"),
            P("req", None),
            P("req", None),
            P(),
            P("tp"),
            P("req", None, "tp"),
            P("req", None, "tp"),
            P("req", "tp", None),
        ),
        out_specs=(P("req", "tp"), P("req", "tp")),
        check_vma=False,
    )
```

```python
import jax
import jax.numpy as jnp
from jax import lax
from jax.sharding import PartitionSpec as P

E = 8
CAP = 128
CHUNKS = 2
RELAY_CHUNKS = ()


epsilon = 1e-05


def rms_norm(values, gain):
    meansq = jnp.mean(values * values, axis=1, keepdims=True)
    return values * lax.rsqrt(meansq + epsilon) * gain[None, :]


def shift_tp(value, step, tp_count):
    return lax.ppermute(value, "tp", [(j, (j + step) % tp_count) for j in range(tp_count)])


def by_source(value, tp_count):
    me = lax.axis_index("tp")
    parts = [value] + [shift_tp(value, s, tp_count) for s in range(1, tp_count)]
    stacked = jnp.stack(parts)
    return jnp.take(stacked, (me - jnp.arange(tp_count)) % tp_count, axis=0)


def gather_tp(value, tp_count):
    me = lax.axis_index("tp")
    rows, cols = value.shape
    whole = jnp.zeros((rows, tp_count * cols), value.dtype)
    for s in range(tp_count):
        part = value if s == 0 else shift_tp(value, s, tp_count)
        whole = lax.dynamic_update_slice_in_dim(whole, part, ((me - s) % tp_count) * cols, axis=1)
    return whole


def sum_tp(value, tp_count):
    ordered = by_source(value, tp_count)
    total = ordered[0]
    for s in range(1, tp_count):
        total = total + ordered[s]
    return total


def down_scatter_sum_tp(activ, w_down, tp_count):
    me = lax.axis_index("tp")
    width = w_down.shape[1] // tp_count
    terms = []
    for s in list(range(1, tp_count)) + [0]:
        w_block = lax.dynamic_slice_in_dim(w_down, ((me + s) % tp_count) * width, width, axis=1)
        block = jnp.dot(activ, w_block, preferred_element_type=jnp.float32).astype(jnp.bfloat16)
        terms.append(block if s == 0 else shift_tp(block, s, tp_count))
    total = terms[0].astype(jnp.float32)
    for term in terms[1:]:
        total = total + term.astype(jnp.float32)
    return total.astype(jnp.bfloat16)


def shards(hidden, routes, route_weights, pre_gain, out_gain, gate_weight, up_weight, down_weight):
    row_count, col_part = hidden.shape
    tp_count = lax.axis_size("tp")
    req_count = lax.axis_size("req")
    full_width = col_part * tp_count
    copies = req_count // E
    slot_count = CAP // copies
    chunk_items = slot_count // CHUNKS
    stream = hidden.astype(jnp.float32)
    whole_rows = gather_tp(hidden, tp_count).astype(jnp.float32)
    normed_in = rms_norm(whole_rows, pre_gain).astype(jnp.bfloat16)
    top = routes.shape[1]
    chosen = routes.reshape(-1)
    onehot = (chosen[:, None] == jnp.arange(E, dtype=jnp.int32)[None, :]).astype(jnp.int32)
    slot_rank = jnp.sum((jnp.cumsum(onehot, axis=0) - 1) * onehot, axis=1)
    dest = (slot_rank % copies) * E + chosen
    item = slot_rank // copies
    chunk_of = item // chunk_items
    in_chunk = dest * chunk_items + item % chunk_items
    chunk_pairs = in_chunk.reshape(row_count, top)
    owner_pairs = chunk_of.reshape(row_count, top)
    slot_ids = jnp.arange(req_count * chunk_items, dtype=jnp.int32)
    returned = []
    for c in range(CHUNKS):
        dispatch = jnp.zeros((req_count * chunk_items, row_count), jnp.bool_)
        for k in range(top):
            hit = (slot_ids[:, None] == chunk_pairs[None, :, k]) & (owner_pairs[None, :, k] == c)
            dispatch = dispatch | hit
        relay = c in RELAY_CHUNKS
        source = hidden if relay else normed_in
        outgoing = jnp.dot(
            dispatch.astype(jnp.bfloat16), source, preferred_element_type=jnp.float32
        ).astype(jnp.bfloat16)
        outgoing = outgoing.reshape(req_count, chunk_items, source.shape[1])
        pieces = lax.all_to_all(outgoing, "req", split_axis=0, concat_axis=0, tiled=True)
        sources, items, widths = pieces.shape
        flat_rows = pieces.reshape(sources * items, widths)
        if relay:
            raw_rows = gather_tp(flat_rows, tp_count).astype(jnp.float32)
            flat_rows = rms_norm(raw_rows, pre_gain).astype(jnp.bfloat16)
        gate_val = jnp.dot(flat_rows, gate_weight[0], preferred_element_type=jnp.float32)
        up_val = jnp.dot(flat_rows, up_weight[0], preferred_element_type=jnp.float32)
        activ = (jax.nn.silu(gate_val) * up_val).astype(jnp.bfloat16)
        summed = down_scatter_sum_tp(activ, down_weight[0], tp_count)
        summed = summed.reshape(sources, items, col_part)
        back = lax.all_to_all(summed, "req", split_axis=0, concat_axis=0, tiled=True)
        returned.append(back.reshape(req_count * chunk_items, col_part))
    total_stream = stream
    for c in range(CHUNKS):
        picked = returned[c][in_chunk].reshape(row_count, top, col_part).astype(jnp.float32)
        mine = (owner_pairs == c)[:, :, None]
        terms = jnp.where(mine, picked * route_weights[:, :, None], 0.0)
        total_stream = total_stream + jnp.sum(terms, axis=1)
    out_sums = sum_tp(jnp.sum(total_stream * total_stream, axis=1), tp_count)
    normed_out = (
        total_stream * lax.rsqrt(out_sums / full_width + epsilon)[:, None] * out_gain[None, :]
    )
    return (total_stream.astype(jnp.bfloat16), normed_out.astype(jnp.bfloat16))


def solution(mesh):
    return jax.shard_map(
        shards,
        mesh=mesh,
        in_specs=(
            P("req", "tp"),
            P("req", None),
            P("req", None),
            P(),
            P("tp"),
            P("req", None, "tp"),
            P("req", None, "tp"),
            P("req", "tp", None),
        ),
        out_specs=(P("req", "tp"), P("req", "tp")),
        check_vma=False,
    )
```

```python
import jax
import jax.numpy as jnp
from jax import lax
from jax.sharding import PartitionSpec as P

E = 8
CAP = 128
CHUNKS = 2


epsilon = 1e-05


def rms_norm(values, gain):
    meansq = jnp.mean(values * values, axis=1, keepdims=True)
    return values * lax.rsqrt(meansq + epsilon) * gain[None, :]


def shift_tp(value, step, tp_count):
    return lax.ppermute(value, "tp", [(j, (j + step) % tp_count) for j in range(tp_count)])


def by_source(value, tp_count):
    me = lax.axis_index("tp")
    parts = [value] + [shift_tp(value, s, tp_count) for s in range(1, tp_count)]
    stacked = jnp.stack(parts)
    return jnp.take(stacked, (me - jnp.arange(tp_count)) % tp_count, axis=0)


def gather_tp(value, tp_count):
    me = lax.axis_index("tp")
    rows, cols = value.shape
    whole = jnp.zeros((rows, tp_count * cols), value.dtype)
    for s in range(tp_count):
        part = value if s == 0 else shift_tp(value, s, tp_count)
        whole = lax.dynamic_update_slice_in_dim(whole, part, ((me - s) % tp_count) * cols, axis=1)
    return whole


def gather_pair_tp(pair, cols, tp_count):
    if tp_count != 4:
        return gather_tp(pair[:, :cols], tp_count)
    me = lax.axis_index("tp")
    own = pair[:, :cols]
    parts = {
        0: own,
        2: pair[:, cols:],
        1: shift_tp(own, 1, tp_count),
        3: shift_tp(own, 3, tp_count),
    }
    whole = jnp.zeros((pair.shape[0], tp_count * cols), pair.dtype)
    for s, part in parts.items():
        whole = lax.dynamic_update_slice_in_dim(whole, part, ((me - s) % tp_count) * cols, axis=1)
    return whole


def sum_tp(value, tp_count):
    ordered = by_source(value, tp_count)
    total = ordered[0]
    for s in range(1, tp_count):
        total = total + ordered[s]
    return total


def down_scatter_sum_tp(activ, w_down, tp_count):
    me = lax.axis_index("tp")
    width = w_down.shape[1] // tp_count
    terms = []
    for s in list(range(1, tp_count)) + [0]:
        w_block = lax.dynamic_slice_in_dim(w_down, ((me + s) % tp_count) * width, width, axis=1)
        block = jnp.dot(activ, w_block, preferred_element_type=jnp.float32).astype(jnp.bfloat16)
        terms.append(block if s == 0 else shift_tp(block, s, tp_count))
    total = terms[0].astype(jnp.float32)
    for term in terms[1:]:
        total = total + term.astype(jnp.float32)
    return total.astype(jnp.bfloat16)


def shards(hidden, routes, route_weights, pre_gain, out_gain, gate_weight, up_weight, down_weight):
    row_count, col_part = hidden.shape
    tp_count = lax.axis_size("tp")
    req_count = lax.axis_size("req")
    full_width = col_part * tp_count
    copies = req_count // E
    slot_count = CAP // copies
    chunk_items = slot_count // CHUNKS
    stream = hidden.astype(jnp.float32)
    whole_raw = gather_tp(hidden, tp_count)
    whole_rows = whole_raw.astype(jnp.float32)
    me = lax.axis_index("tp")
    far_cols = ((me + tp_count // 2) % tp_count) * col_part
    pair_raw = jnp.concatenate(
        [hidden, lax.dynamic_slice_in_dim(whole_raw, far_cols, col_part, axis=1)], axis=1
    )
    normed_in = rms_norm(whole_rows, pre_gain).astype(jnp.bfloat16)
    top = routes.shape[1]
    chosen = routes.reshape(-1)
    onehot = (chosen[:, None] == jnp.arange(E, dtype=jnp.int32)[None, :]).astype(jnp.int32)
    slot_rank = jnp.sum((jnp.cumsum(onehot, axis=0) - 1) * onehot, axis=1)
    dest = (slot_rank % copies) * E + chosen
    item = slot_rank // copies
    chunk_of = item // chunk_items
    in_chunk = dest * chunk_items + item % chunk_items
    chunk_pairs = in_chunk.reshape(row_count, top)
    owner_pairs = chunk_of.reshape(row_count, top)
    slot_ids = jnp.arange(req_count * chunk_items, dtype=jnp.int32)
    returned = []
    for c in range(CHUNKS):
        dispatch = jnp.zeros((req_count * chunk_items, row_count), jnp.bool_)
        for k in range(top):
            hit = (slot_ids[:, None] == chunk_pairs[None, :, k]) & (owner_pairs[None, :, k] == c)
            dispatch = dispatch | hit
        relay = c == 0
        source = pair_raw if relay else normed_in
        outgoing = jnp.dot(
            dispatch.astype(jnp.bfloat16), source, preferred_element_type=jnp.float32
        ).astype(jnp.bfloat16)
        outgoing = outgoing.reshape(req_count, chunk_items, source.shape[1])
        pieces = lax.all_to_all(outgoing, "req", split_axis=0, concat_axis=0, tiled=True)
        sources, items, widths = pieces.shape
        flat_rows = pieces.reshape(sources * items, widths)
        if relay:
            raw_rows = gather_pair_tp(flat_rows, col_part, tp_count).astype(jnp.float32)
            flat_rows = rms_norm(raw_rows, pre_gain).astype(jnp.bfloat16)
        gate_val = jnp.dot(flat_rows, gate_weight[0], preferred_element_type=jnp.float32)
        up_val = jnp.dot(flat_rows, up_weight[0], preferred_element_type=jnp.float32)
        activ = (jax.nn.silu(gate_val) * up_val).astype(jnp.bfloat16)
        summed = down_scatter_sum_tp(activ, down_weight[0], tp_count)
        summed = summed.reshape(sources, items, col_part)
        back = lax.all_to_all(summed, "req", split_axis=0, concat_axis=0, tiled=True)
        returned.append(back.reshape(req_count * chunk_items, col_part))
    total_stream = stream
    for c in range(CHUNKS):
        picked = returned[c][in_chunk].reshape(row_count, top, col_part).astype(jnp.float32)
        mine = (owner_pairs == c)[:, :, None]
        terms = jnp.where(mine, picked * route_weights[:, :, None], 0.0)
        total_stream = total_stream + jnp.sum(terms, axis=1)
    out_sums = sum_tp(jnp.sum(total_stream * total_stream, axis=1), tp_count)
    normed_out = (
        total_stream * lax.rsqrt(out_sums / full_width + epsilon)[:, None] * out_gain[None, :]
    )
    return (total_stream.astype(jnp.bfloat16), normed_out.astype(jnp.bfloat16))


def solution(mesh):
    return jax.shard_map(
        shards,
        mesh=mesh,
        in_specs=(
            P("req", "tp"),
            P("req", None),
            P("req", None),
            P(),
            P("tp"),
            P("req", None, "tp"),
            P("req", None, "tp"),
            P("req", "tp", None),
        ),
        out_specs=(P("req", "tp"), P("req", "tp")),
        check_vma=False,
    )
```

```python
import jax
import jax.numpy as jnp
from jax import lax
from jax.sharding import PartitionSpec as P

E = 8
CAP = 128
CHUNKS = 2


epsilon = 1e-05


def rms_norm(values, gain):
    meansq = jnp.mean(values * values, axis=1, keepdims=True)
    return values * lax.rsqrt(meansq + epsilon) * gain[None, :]


def shift_tp(value, step, tp_count):
    return lax.ppermute(value, "tp", [(j, (j + step) % tp_count) for j in range(tp_count)])


def by_source(value, tp_count):
    me = lax.axis_index("tp")
    parts = [value] + [shift_tp(value, s, tp_count) for s in range(1, tp_count)]
    stacked = jnp.stack(parts)
    return jnp.take(stacked, (me - jnp.arange(tp_count)) % tp_count, axis=0)


def gather_tp(value, tp_count):
    me = lax.axis_index("tp")
    rows, cols = value.shape
    whole = jnp.zeros((rows, tp_count * cols), value.dtype)
    for s in range(tp_count):
        part = value if s == 0 else shift_tp(value, s, tp_count)
        whole = lax.dynamic_update_slice_in_dim(whole, part, ((me - s) % tp_count) * cols, axis=1)
    return whole


def sum_tp(value, tp_count):
    ordered = by_source(value, tp_count)
    total = ordered[0]
    for s in range(1, tp_count):
        total = total + ordered[s]
    return total


def down_scatter_sum_tp(activ, w_down, tp_count):
    me = lax.axis_index("tp")
    width = w_down.shape[1] // tp_count
    terms = []
    for s in list(range(1, tp_count)) + [0]:
        w_block = lax.dynamic_slice_in_dim(w_down, ((me + s) % tp_count) * width, width, axis=1)
        block = jnp.dot(activ, w_block, preferred_element_type=jnp.float32).astype(jnp.bfloat16)
        terms.append(block if s == 0 else shift_tp(block, s, tp_count))
    total = terms[0].astype(jnp.float32)
    for term in terms[1:]:
        total = total + term.astype(jnp.float32)
    return total.astype(jnp.bfloat16)


def shards(hidden, routes, route_weights, pre_gain, out_gain, gate_weight, up_weight, down_weight):
    row_count, col_part = hidden.shape
    tp_count = lax.axis_size("tp")
    req_count = lax.axis_size("req")
    full_width = col_part * tp_count
    copies = req_count // E
    slot_count = CAP // copies
    chunk_items = slot_count // CHUNKS
    stream = hidden.astype(jnp.float32)
    whole_rows = gather_tp(hidden, tp_count).astype(jnp.float32)
    normed_in = rms_norm(whole_rows, pre_gain).astype(jnp.bfloat16)
    top = routes.shape[1]
    chosen = routes.reshape(-1)
    onehot = (chosen[:, None] == jnp.arange(E, dtype=jnp.int32)[None, :]).astype(jnp.int32)
    slot_rank = jnp.sum((jnp.cumsum(onehot, axis=0) - 1) * onehot, axis=1)
    dest = (slot_rank % copies) * E + chosen
    item = slot_rank // copies
    chunk_of = item // chunk_items
    in_chunk = dest * chunk_items + item % chunk_items
    chunk_pairs = in_chunk.reshape(row_count, top)
    owner_pairs = chunk_of.reshape(row_count, top)
    slot_ids = jnp.arange(req_count * chunk_items, dtype=jnp.int32)
    returned = []
    for c in range(CHUNKS):
        dispatch = jnp.zeros((req_count * chunk_items, row_count), jnp.bool_)
        for k in range(top):
            hit = (slot_ids[:, None] == chunk_pairs[None, :, k]) & (owner_pairs[None, :, k] == c)
            dispatch = dispatch | hit
        relay = c == 0
        source = hidden if relay else normed_in
        outgoing = jnp.dot(
            dispatch.astype(jnp.bfloat16), source, preferred_element_type=jnp.float32
        ).astype(jnp.bfloat16)
        outgoing = outgoing.reshape(req_count, chunk_items, source.shape[1])
        pieces = lax.all_to_all(outgoing, "req", split_axis=0, concat_axis=0, tiled=True)
        sources, items, widths = pieces.shape
        flat_rows = pieces.reshape(sources * items, widths)
        if relay:
            raw_rows = gather_tp(flat_rows, tp_count).astype(jnp.float32)
            flat_rows = rms_norm(raw_rows, pre_gain).astype(jnp.bfloat16)
        gate_val = jnp.dot(flat_rows, gate_weight[0], preferred_element_type=jnp.float32)
        up_val = jnp.dot(flat_rows, up_weight[0], preferred_element_type=jnp.float32)
        activ = (jax.nn.silu(gate_val) * up_val).astype(jnp.bfloat16)
        summed = down_scatter_sum_tp(activ, down_weight[0], tp_count)
        summed = summed.reshape(sources, items, col_part)
        back = lax.all_to_all(summed, "req", split_axis=0, concat_axis=0, tiled=True)
        returned.append(back.reshape(req_count * chunk_items, col_part))
    weight_hi = route_weights.astype(jnp.bfloat16)
    weight_lo = (route_weights - weight_hi.astype(jnp.float32)).astype(jnp.bfloat16)
    total_stream = stream
    for c in range(CHUNKS):
        combine_hi = jnp.zeros((row_count, req_count * chunk_items), jnp.bfloat16)
        combine_lo = jnp.zeros((row_count, req_count * chunk_items), jnp.bfloat16)
        for k in range(top):
            hit = (chunk_pairs[:, k][:, None] == slot_ids[None, :]) & (owner_pairs[:, k][:, None] == c)
            combine_hi = jnp.where(hit, weight_hi[:, k][:, None], combine_hi)
            combine_lo = jnp.where(hit, weight_lo[:, k][:, None], combine_lo)
        mixed = jnp.dot(combine_hi, returned[c], preferred_element_type=jnp.float32)
        mixed = mixed + jnp.dot(combine_lo, returned[c], preferred_element_type=jnp.float32)
        total_stream = total_stream + mixed
    out_sums = sum_tp(jnp.sum(total_stream * total_stream, axis=1), tp_count)
    normed_out = (
        total_stream * lax.rsqrt(out_sums / full_width + epsilon)[:, None] * out_gain[None, :]
    )
    return (total_stream.astype(jnp.bfloat16), normed_out.astype(jnp.bfloat16))


def solution(mesh):
    return jax.shard_map(
        shards,
        mesh=mesh,
        in_specs=(
            P("req", "tp"),
            P("req", None),
            P("req", None),
            P(),
            P("tp"),
            P("req", None, "tp"),
            P("req", None, "tp"),
            P("req", "tp", None),
        ),
        out_specs=(P("req", "tp"), P("req", "tp")),
        check_vma=False,
    )
```

```python
import jax
import jax.numpy as jnp
from jax import lax
from jax.sharding import PartitionSpec as P

E = 8
CAP = 128
CHUNKS = 2


epsilon = 1e-05


def rms_norm(values, gain):
    meansq = jnp.mean(values * values, axis=1, keepdims=True)
    return values * lax.rsqrt(meansq + epsilon) * gain[None, :]


def shift_tp(value, step, tp_count):
    return lax.ppermute(value, "tp", [(j, (j + step) % tp_count) for j in range(tp_count)])


def by_source(value, tp_count):
    me = lax.axis_index("tp")
    parts = [value] + [shift_tp(value, s, tp_count) for s in range(1, tp_count)]
    stacked = jnp.stack(parts)
    return jnp.take(stacked, (me - jnp.arange(tp_count)) % tp_count, axis=0)


def gather_tp(value, tp_count, known=None):
    me = lax.axis_index("tp")
    rows, cols = value.shape
    whole = jnp.zeros((rows, tp_count * cols), value.dtype)
    for s in range(tp_count):
        part = (known or {}).get(s)
        if part is None:
            part = value if s == 0 else shift_tp(value, s, tp_count)
        whole = lax.dynamic_update_slice_in_dim(whole, part, ((me - s) % tp_count) * cols, axis=1)
    return whole


def gather_pair_tp(pair, cols, tp_count):
    me = lax.axis_index("tp")
    own = pair[:, :cols]
    parts = {0: own, 2: pair[:, cols:], 1: shift_tp(own, 1, tp_count), 3: shift_tp(own, 3, tp_count)}
    whole = jnp.zeros((pair.shape[0], tp_count * cols), pair.dtype)
    for s, part in parts.items():
        whole = lax.dynamic_update_slice_in_dim(whole, part, ((me - s) % tp_count) * cols, axis=1)
    return whole


def sum_tp(value, tp_count):
    ordered = by_source(value, tp_count)
    total = ordered[0]
    for s in range(1, tp_count):
        total = total + ordered[s]
    return total


def down_scatter_sum_tp(activ, w_down, tp_count):
    me = lax.axis_index("tp")
    width = w_down.shape[1] // tp_count
    terms = []
    for s in list(range(1, tp_count)) + [0]:
        w_block = lax.dynamic_slice_in_dim(w_down, ((me + s) % tp_count) * width, width, axis=1)
        block = jnp.dot(activ, w_block, preferred_element_type=jnp.float32).astype(jnp.bfloat16)
        terms.append(block if s == 0 else shift_tp(block, s, tp_count))
    total = terms[0].astype(jnp.float32)
    for term in terms[1:]:
        total = total + term.astype(jnp.float32)
    return total.astype(jnp.bfloat16)


def shards(hidden, routes, route_weights, pre_gain, out_gain, gate_weight, up_weight, down_weight):
    row_count, col_part = hidden.shape
    tp_count = lax.axis_size("tp")
    req_count = lax.axis_size("req")
    full_width = col_part * tp_count
    copies = req_count // E
    slot_count = CAP // copies
    chunk_items = slot_count // CHUNKS
    stream = hidden.astype(jnp.float32)
    me = lax.axis_index("tp")
    half_turn = tp_count // 2
    far = shift_tp(hidden, half_turn, tp_count) if tp_count == 4 else None
    whole_rows = gather_tp(hidden, tp_count, {half_turn: far}).astype(jnp.float32)
    normed_in = rms_norm(whole_rows, pre_gain).astype(jnp.bfloat16)
    top = routes.shape[1]
    chosen = routes.reshape(-1)
    onehot = (chosen[:, None] == jnp.arange(E, dtype=jnp.int32)[None, :]).astype(jnp.int32)
    slot_rank = jnp.sum((jnp.cumsum(onehot, axis=0) - 1) * onehot, axis=1)
    dest = (slot_rank % copies) * E + chosen
    item = slot_rank // copies
    chunk_of = item // chunk_items
    in_chunk = dest * chunk_items + item % chunk_items
    chunk_pairs = in_chunk.reshape(row_count, top)
    owner_pairs = chunk_of.reshape(row_count, top)
    slot_ids = jnp.arange(req_count * chunk_items, dtype=jnp.int32)
    returned = []
    for c in range(CHUNKS):
        dispatch = jnp.zeros((req_count * chunk_items, row_count), jnp.bool_)
        for k in range(top):
            hit = (slot_ids[:, None] == chunk_pairs[None, :, k]) & (owner_pairs[None, :, k] == c)
            dispatch = dispatch | hit
        relay = c == 0
        source = hidden if far is None else jnp.concatenate([hidden, far], axis=1)
        source = source if relay else normed_in
        outgoing = jnp.dot(
            dispatch.astype(jnp.bfloat16), source, preferred_element_type=jnp.float32
        ).astype(jnp.bfloat16)
        outgoing = outgoing.reshape(req_count, chunk_items, source.shape[1])
        pieces = lax.all_to_all(outgoing, "req", split_axis=0, concat_axis=0, tiled=True)
        sources, items, widths = pieces.shape
        flat_rows = pieces.reshape(sources * items, widths)
        if relay:
            if far is not None:
                raw_rows = gather_pair_tp(flat_rows, col_part, tp_count)
            else:
                raw_rows = gather_tp(flat_rows, tp_count)
            flat_rows = rms_norm(raw_rows.astype(jnp.float32), pre_gain).astype(jnp.bfloat16)
        gate_val = jnp.dot(flat_rows, gate_weight[0], preferred_element_type=jnp.float32)
        up_val = jnp.dot(flat_rows, up_weight[0], preferred_element_type=jnp.float32)
        activ = (jax.nn.silu(gate_val) * up_val).astype(jnp.bfloat16)
        summed = down_scatter_sum_tp(activ, down_weight[0], tp_count)
        summed = summed.reshape(sources, items, col_part)
        back = lax.all_to_all(summed, "req", split_axis=0, concat_axis=0, tiled=True)
        returned.append(back.reshape(req_count * chunk_items, col_part))
    weight_hi = route_weights.astype(jnp.bfloat16)
    weight_lo = (route_weights - weight_hi.astype(jnp.float32)).astype(jnp.bfloat16)
    total_stream = stream
    for c in range(CHUNKS):
        combine_hi = jnp.zeros((row_count, req_count * chunk_items), jnp.bfloat16)
        combine_lo = jnp.zeros((row_count, req_count * chunk_items), jnp.bfloat16)
        for k in range(top):
            hit = (chunk_pairs[:, k][:, None] == slot_ids[None, :]) & (owner_pairs[:, k][:, None] == c)
            combine_hi = jnp.where(hit, weight_hi[:, k][:, None], combine_hi)
            combine_lo = jnp.where(hit, weight_lo[:, k][:, None], combine_lo)
        mixed = jnp.dot(combine_hi, returned[c], preferred_element_type=jnp.float32)
        mixed = mixed + jnp.dot(combine_lo, returned[c], preferred_element_type=jnp.float32)
        total_stream = total_stream + mixed
    out_sums = sum_tp(jnp.sum(total_stream * total_stream, axis=1), tp_count)
    normed_out = (
        total_stream * lax.rsqrt(out_sums / full_width + epsilon)[:, None] * out_gain[None, :]
    )
    return (total_stream.astype(jnp.bfloat16), normed_out.astype(jnp.bfloat16))


def solution(mesh):
    return jax.shard_map(
        shards,
        mesh=mesh,
        in_specs=(
            P("req", "tp"),
            P("req", None),
            P("req", None),
            P(),
            P("tp"),
            P("req", None, "tp"),
            P("req", None, "tp"),
            P("req", "tp", None),
        ),
        out_specs=(P("req", "tp"), P("req", "tp")),
        check_vma=False,
    )
```

```python
import jax
import jax.numpy as jnp
from jax import lax
from jax.sharding import PartitionSpec as P

E = 8
CAP = 128
CHUNKS = 2


epsilon = 1e-05


def rms_norm(values, gain):
    meansq = jnp.mean(values * values, axis=1, keepdims=True)
    return values * lax.rsqrt(meansq + epsilon) * gain[None, :]


def shift_tp(value, step, tp_count):
    return lax.ppermute(value, "tp", [(j, (j + step) % tp_count) for j in range(tp_count)])


def by_source(value, tp_count):
    me = lax.axis_index("tp")
    parts = [value] + [shift_tp(value, s, tp_count) for s in range(1, tp_count)]
    stacked = jnp.stack(parts)
    return jnp.take(stacked, (me - jnp.arange(tp_count)) % tp_count, axis=0)


def gather_tp(value, tp_count, known=None):
    me = lax.axis_index("tp")
    rows, cols = value.shape
    whole = jnp.zeros((rows, tp_count * cols), value.dtype)
    for s in range(tp_count):
        part = (known or {}).get(s)
        if part is None:
            part = value if s == 0 else shift_tp(value, s, tp_count)
        whole = lax.dynamic_update_slice_in_dim(whole, part, ((me - s) % tp_count) * cols, axis=1)
    return whole


def gather_pair_tp(pair, cols, tp_count):
    me = lax.axis_index("tp")
    own = pair[:, :cols]
    parts = {0: own, 2: pair[:, cols:], 1: shift_tp(own, 1, tp_count), 3: shift_tp(own, 3, tp_count)}
    whole = jnp.zeros((pair.shape[0], tp_count * cols), pair.dtype)
    for s, part in parts.items():
        whole = lax.dynamic_update_slice_in_dim(whole, part, ((me - s) % tp_count) * cols, axis=1)
    return whole


def sum_tp(value, tp_count):
    ordered = by_source(value, tp_count)
    total = ordered[0]
    for s in range(1, tp_count):
        total = total + ordered[s]
    return total


def down_scatter_sum_tp(activ, w_down, tp_count):
    me = lax.axis_index("tp")
    width = w_down.shape[1] // tp_count
    terms = []
    for s in list(range(1, tp_count)) + [0]:
        w_block = lax.dynamic_slice_in_dim(w_down, ((me + s) % tp_count) * width, width, axis=1)
        block = jnp.dot(activ, w_block, preferred_element_type=jnp.float32).astype(jnp.bfloat16)
        terms.append(block if s == 0 else shift_tp(block, s, tp_count))
    total = terms[0].astype(jnp.float32)
    for term in terms[1:]:
        total = total + term.astype(jnp.float32)
    return total.astype(jnp.bfloat16)


def shards(hidden, routes, route_weights, pre_gain, out_gain, gate_weight, up_weight, down_weight):
    row_count, col_part = hidden.shape
    tp_count = lax.axis_size("tp")
    req_count = lax.axis_size("req")
    full_width = col_part * tp_count
    copies = req_count // E
    slot_count = CAP // copies
    first_items = slot_count * 3 // 8
    chunk_sizes = [first_items, slot_count - first_items]
    chunk_starts = [0, first_items]
    stream = hidden.astype(jnp.float32)
    me = lax.axis_index("tp")
    half_turn = tp_count // 2
    far = shift_tp(hidden, half_turn, tp_count) if tp_count == 4 else None
    whole_rows = gather_tp(hidden, tp_count, {half_turn: far}).astype(jnp.float32)
    normed_in = rms_norm(whole_rows, pre_gain).astype(jnp.bfloat16)
    top = routes.shape[1]
    chosen = routes.reshape(-1)
    onehot = (chosen[:, None] == jnp.arange(E, dtype=jnp.int32)[None, :]).astype(jnp.int32)
    slot_rank = jnp.sum((jnp.cumsum(onehot, axis=0) - 1) * onehot, axis=1)
    dest = (slot_rank % copies) * E + chosen
    item = slot_rank // copies
    chunk_of = (item >= chunk_starts[1]).astype(jnp.int32)
    in_chunk = jnp.where(
        chunk_of == 0, dest * chunk_sizes[0] + item, dest * chunk_sizes[1] + item - chunk_starts[1]
    )
    chunk_pairs = in_chunk.reshape(row_count, top)
    owner_pairs = chunk_of.reshape(row_count, top)
    returned = []
    for c in range(CHUNKS):
        chunk_items = chunk_sizes[c]
        slot_ids = jnp.arange(req_count * chunk_items, dtype=jnp.int32)
        dispatch = jnp.zeros((req_count * chunk_items, row_count), jnp.bool_)
        for k in range(top):
            hit = (slot_ids[:, None] == chunk_pairs[None, :, k]) & (owner_pairs[None, :, k] == c)
            dispatch = dispatch | hit
        relay = c == 0
        source = hidden if far is None else jnp.concatenate([hidden, far], axis=1)
        source = source if relay else normed_in
        outgoing = jnp.dot(
            dispatch.astype(jnp.bfloat16), source, preferred_element_type=jnp.float32
        ).astype(jnp.bfloat16)
        outgoing = outgoing.reshape(req_count, chunk_items, source.shape[1])
        pieces = lax.all_to_all(outgoing, "req", split_axis=0, concat_axis=0, tiled=True)
        sources, items, widths = pieces.shape
        flat_rows = pieces.reshape(sources * items, widths)
        if relay:
            if far is not None:
                raw_rows = gather_pair_tp(flat_rows, col_part, tp_count)
            else:
                raw_rows = gather_tp(flat_rows, tp_count)
            flat_rows = rms_norm(raw_rows.astype(jnp.float32), pre_gain).astype(jnp.bfloat16)
        gate_val = jnp.dot(flat_rows, gate_weight[0], preferred_element_type=jnp.float32)
        up_val = jnp.dot(flat_rows, up_weight[0], preferred_element_type=jnp.float32)
        activ = (jax.nn.silu(gate_val) * up_val).astype(jnp.bfloat16)
        summed = down_scatter_sum_tp(activ, down_weight[0], tp_count)
        summed = summed.reshape(sources, items, col_part)
        back = lax.all_to_all(summed, "req", split_axis=0, concat_axis=0, tiled=True)
        returned.append(back.reshape(req_count * chunk_items, col_part))
    weight_hi = route_weights.astype(jnp.bfloat16)
    weight_lo = (route_weights - weight_hi.astype(jnp.float32)).astype(jnp.bfloat16)
    total_stream = stream
    for c in range(CHUNKS):
        slot_ids = jnp.arange(req_count * chunk_sizes[c], dtype=jnp.int32)
        combine_hi = jnp.zeros((row_count, req_count * chunk_sizes[c]), jnp.bfloat16)
        combine_lo = jnp.zeros((row_count, req_count * chunk_sizes[c]), jnp.bfloat16)
        for k in range(top):
            hit = (chunk_pairs[:, k][:, None] == slot_ids[None, :]) & (owner_pairs[:, k][:, None] == c)
            combine_hi = jnp.where(hit, weight_hi[:, k][:, None], combine_hi)
            combine_lo = jnp.where(hit, weight_lo[:, k][:, None], combine_lo)
        mixed = jnp.dot(combine_hi, returned[c], preferred_element_type=jnp.float32)
        mixed = mixed + jnp.dot(combine_lo, returned[c], preferred_element_type=jnp.float32)
        total_stream = total_stream + mixed
    out_sums = sum_tp(jnp.sum(total_stream * total_stream, axis=1), tp_count)
    normed_out = (
        total_stream * lax.rsqrt(out_sums / full_width + epsilon)[:, None] * out_gain[None, :]
    )
    return (total_stream.astype(jnp.bfloat16), normed_out.astype(jnp.bfloat16))


def solution(mesh):
    return jax.shard_map(
        shards,
        mesh=mesh,
        in_specs=(
            P("req", "tp"),
            P("req", None),
            P("req", None),
            P(),
            P("tp"),
            P("req", None, "tp"),
            P("req", None, "tp"),
            P("req", "tp", None),
        ),
        out_specs=(P("req", "tp"), P("req", "tp")),
        check_vma=False,
    )
```

```python
import jax
import jax.numpy as jnp
from jax import lax
from jax.sharding import PartitionSpec as P

E = 8
CAP = 128
CHUNKS = 2


epsilon = 1e-05


def rms_norm(values, gain):
    meansq = jnp.mean(values * values, axis=1, keepdims=True)
    return values * lax.rsqrt(meansq + epsilon) * gain[None, :]


def shift_tp(value, step, tp_count):
    return lax.ppermute(value, "tp", [(j, (j + step) % tp_count) for j in range(tp_count)])


def by_source(value, tp_count):
    me = lax.axis_index("tp")
    parts = [value] + [shift_tp(value, s, tp_count) for s in range(1, tp_count)]
    stacked = jnp.stack(parts)
    return jnp.take(stacked, (me - jnp.arange(tp_count)) % tp_count, axis=0)


def gather_tp(value, tp_count, known=None):
    me = lax.axis_index("tp")
    rows, cols = value.shape
    whole = jnp.zeros((rows, tp_count * cols), value.dtype)
    for s in range(tp_count):
        part = (known or {}).get(s)
        if part is None:
            part = value if s == 0 else shift_tp(value, s, tp_count)
        whole = lax.dynamic_update_slice_in_dim(whole, part, ((me - s) % tp_count) * cols, axis=1)
    return whole


def gather_pair_tp(pair, cols, tp_count):
    me = lax.axis_index("tp")
    own = pair[:, :cols]
    parts = {0: own, 2: pair[:, cols:], 1: shift_tp(own, 1, tp_count), 3: shift_tp(own, 3, tp_count)}
    whole = jnp.zeros((pair.shape[0], tp_count * cols), pair.dtype)
    for s, part in parts.items():
        whole = lax.dynamic_update_slice_in_dim(whole, part, ((me - s) % tp_count) * cols, axis=1)
    return whole


def sum_tp(value, tp_count):
    ordered = by_source(value, tp_count)
    total = ordered[0]
    for s in range(1, tp_count):
        total = total + ordered[s]
    return total


def down_scatter_sum_tp(activ, w_down, tp_count):
    me = lax.axis_index("tp")
    width = w_down.shape[1] // tp_count
    far = tp_count // 2
    order = [far] + [s for s in range(1, tp_count) if s != far] + [0]
    terms = {}
    for s in order:
        w_block = lax.dynamic_slice_in_dim(w_down, ((me + s) % tp_count) * width, width, axis=1)
        block = jnp.dot(activ, w_block, preferred_element_type=jnp.float32).astype(jnp.bfloat16)
        terms[s] = block if s == 0 else shift_tp(block, s, tp_count)
    near = terms[0].astype(jnp.float32)
    for s in order[1:-1]:
        near = near + terms[s].astype(jnp.float32)
    near = lax.optimization_barrier(near)
    return (near + terms[far].astype(jnp.float32)).astype(jnp.bfloat16)


def shards(hidden, routes, route_weights, pre_gain, out_gain, gate_weight, up_weight, down_weight):
    row_count, col_part = hidden.shape
    tp_count = lax.axis_size("tp")
    req_count = lax.axis_size("req")
    full_width = col_part * tp_count
    copies = req_count // E
    slot_count = CAP // copies
    chunk_items = slot_count // CHUNKS
    stream = hidden.astype(jnp.float32)
    me = lax.axis_index("tp")
    half_turn = tp_count // 2
    far = shift_tp(hidden, half_turn, tp_count) if tp_count == 4 else None
    whole_rows = gather_tp(hidden, tp_count, {half_turn: far}).astype(jnp.float32)
    normed_in = rms_norm(whole_rows, pre_gain).astype(jnp.bfloat16)
    top = routes.shape[1]
    chosen = routes.reshape(-1)
    onehot = (chosen[:, None] == jnp.arange(E, dtype=jnp.int32)[None, :]).astype(jnp.int32)
    slot_rank = jnp.sum((jnp.cumsum(onehot, axis=0) - 1) * onehot, axis=1)
    dest = (slot_rank % copies) * E + chosen
    item = slot_rank // copies
    chunk_of = item // chunk_items
    in_chunk = dest * chunk_items + item % chunk_items
    chunk_pairs = in_chunk.reshape(row_count, top)
    owner_pairs = chunk_of.reshape(row_count, top)
    slot_ids = jnp.arange(req_count * chunk_items, dtype=jnp.int32)
    returned = []
    for c in range(CHUNKS):
        dispatch = jnp.zeros((req_count * chunk_items, row_count), jnp.bool_)
        for k in range(top):
            hit = (slot_ids[:, None] == chunk_pairs[None, :, k]) & (owner_pairs[None, :, k] == c)
            dispatch = dispatch | hit
        relay = c == 0
        source = hidden if far is None else jnp.concatenate([hidden, far], axis=1)
        source = source if relay else normed_in
        outgoing = jnp.dot(
            dispatch.astype(jnp.bfloat16), source, preferred_element_type=jnp.float32
        ).astype(jnp.bfloat16)
        outgoing = outgoing.reshape(req_count, chunk_items, source.shape[1])
        pieces = lax.all_to_all(outgoing, "req", split_axis=0, concat_axis=0, tiled=True)
        sources, items, widths = pieces.shape
        flat_rows = pieces.reshape(sources * items, widths)
        if relay:
            if far is not None:
                raw_rows = gather_pair_tp(flat_rows, col_part, tp_count)
            else:
                raw_rows = gather_tp(flat_rows, tp_count)
            flat_rows = rms_norm(raw_rows.astype(jnp.float32), pre_gain).astype(jnp.bfloat16)
        gate_val = jnp.dot(flat_rows, gate_weight[0], preferred_element_type=jnp.float32)
        up_val = jnp.dot(flat_rows, up_weight[0], preferred_element_type=jnp.float32)
        activ = (jax.nn.silu(gate_val) * up_val).astype(jnp.bfloat16)
        summed = down_scatter_sum_tp(activ, down_weight[0], tp_count)
        summed = summed.reshape(sources, items, col_part)
        back = lax.all_to_all(summed, "req", split_axis=0, concat_axis=0, tiled=True)
        returned.append(back.reshape(req_count * chunk_items, col_part))
    weight_hi = route_weights.astype(jnp.bfloat16)
    weight_lo = (route_weights - weight_hi.astype(jnp.float32)).astype(jnp.bfloat16)
    total_stream = stream
    for c in range(CHUNKS):
        combine_hi = jnp.zeros((row_count, req_count * chunk_items), jnp.bfloat16)
        combine_lo = jnp.zeros((row_count, req_count * chunk_items), jnp.bfloat16)
        for k in range(top):
            hit = (chunk_pairs[:, k][:, None] == slot_ids[None, :]) & (owner_pairs[:, k][:, None] == c)
            combine_hi = jnp.where(hit, weight_hi[:, k][:, None], combine_hi)
            combine_lo = jnp.where(hit, weight_lo[:, k][:, None], combine_lo)
        mixed = jnp.dot(combine_hi, returned[c], preferred_element_type=jnp.float32)
        mixed = mixed + jnp.dot(combine_lo, returned[c], preferred_element_type=jnp.float32)
        total_stream = total_stream + mixed
    out_sums = sum_tp(jnp.sum(total_stream * total_stream, axis=1), tp_count)
    normed_out = (
        total_stream * lax.rsqrt(out_sums / full_width + epsilon)[:, None] * out_gain[None, :]
    )
    return (total_stream.astype(jnp.bfloat16), normed_out.astype(jnp.bfloat16))


def solution(mesh):
    return jax.shard_map(
        shards,
        mesh=mesh,
        in_specs=(
            P("req", "tp"),
            P("req", None),
            P("req", None),
            P(),
            P("tp"),
            P("req", None, "tp"),
            P("req", None, "tp"),
            P("req", "tp", None),
        ),
        out_specs=(P("req", "tp"), P("req", "tp")),
        check_vma=False,
    )
```

```python
import jax
import jax.numpy as jnp
from jax import lax
from jax.sharding import PartitionSpec as P

E = 8
CAP = 128
CHUNKS = 2


epsilon = 1e-05


def rms_norm(values, gain):
    meansq = jnp.mean(values * values, axis=1, keepdims=True)
    return values * lax.rsqrt(meansq + epsilon) * gain[None, :]


def shift_tp(value, step, tp_count):
    return lax.ppermute(value, "tp", [(j, (j + step) % tp_count) for j in range(tp_count)])


def by_source(value, tp_count):
    me = lax.axis_index("tp")
    parts = [value] + [shift_tp(value, s, tp_count) for s in range(1, tp_count)]
    stacked = jnp.stack(parts)
    return jnp.take(stacked, (me - jnp.arange(tp_count)) % tp_count, axis=0)


def gather_tp(value, tp_count, known=None):
    me = lax.axis_index("tp")
    rows, cols = value.shape
    whole = jnp.zeros((rows, tp_count * cols), value.dtype)
    for s in range(tp_count):
        part = (known or {}).get(s)
        if part is None:
            part = value if s == 0 else shift_tp(value, s, tp_count)
        whole = lax.dynamic_update_slice_in_dim(whole, part, ((me - s) % tp_count) * cols, axis=1)
    return whole


def gather_pair_tp(pair, cols, tp_count):
    me = lax.axis_index("tp")
    own = pair[:, :cols]
    parts = {0: own, 2: pair[:, cols:], 1: shift_tp(own, 1, tp_count), 3: shift_tp(own, 3, tp_count)}
    whole = jnp.zeros((pair.shape[0], tp_count * cols), pair.dtype)
    for s, part in parts.items():
        whole = lax.dynamic_update_slice_in_dim(whole, part, ((me - s) % tp_count) * cols, axis=1)
    return whole


def sum_tp(value, tp_count):
    ordered = by_source(value, tp_count)
    total = ordered[0]
    for s in range(1, tp_count):
        total = total + ordered[s]
    return total


def down_scatter_sum_tp(activ, w_down, tp_count):
    me = lax.axis_index("tp")
    width = w_down.shape[1] // tp_count
    terms = []
    for s in list(range(1, tp_count)) + [0]:
        w_block = lax.dynamic_slice_in_dim(w_down, ((me + s) % tp_count) * width, width, axis=1)
        block = jnp.dot(activ, w_block, preferred_element_type=jnp.float32).astype(jnp.bfloat16)
        terms.append(block if s == 0 else shift_tp(block, s, tp_count))
    total = terms[0].astype(jnp.float32)
    for term in terms[1:]:
        total = total + term.astype(jnp.float32)
    return total.astype(jnp.bfloat16)


def shards(hidden, routes, route_weights, pre_gain, out_gain, gate_weight, up_weight, down_weight):
    row_count, col_part = hidden.shape
    tp_count = lax.axis_size("tp")
    req_count = lax.axis_size("req")
    full_width = col_part * tp_count
    copies = req_count // E
    slot_count = CAP // copies
    chunk_items = slot_count // CHUNKS
    stream = hidden.astype(jnp.float32)
    me = lax.axis_index("tp")
    half_turn = tp_count // 2
    far = shift_tp(hidden, half_turn, tp_count) if tp_count == 4 else None
    normed_in = None
    top = routes.shape[1]
    chosen = routes.reshape(-1)
    onehot = (chosen[:, None] == jnp.arange(E, dtype=jnp.int32)[None, :]).astype(jnp.int32)
    slot_rank = jnp.sum((jnp.cumsum(onehot, axis=0) - 1) * onehot, axis=1)
    dest = (slot_rank % copies) * E + chosen
    item = slot_rank // copies
    chunk_of = item // chunk_items
    in_chunk = dest * chunk_items + item % chunk_items
    chunk_pairs = in_chunk.reshape(row_count, top)
    owner_pairs = chunk_of.reshape(row_count, top)
    slot_ids = jnp.arange(req_count * chunk_items, dtype=jnp.int32)
    returned = []
    anchor = None
    for c in range(CHUNKS):
        dispatch = jnp.zeros((req_count * chunk_items, row_count), jnp.bool_)
        for k in range(top):
            hit = (slot_ids[:, None] == chunk_pairs[None, :, k]) & (owner_pairs[None, :, k] == c)
            dispatch = dispatch | hit
        relay = c == 0
        source = hidden if far is None else jnp.concatenate([hidden, far], axis=1)
        if not relay and normed_in is None:
            late = hidden if anchor is None else lax.optimization_barrier((hidden, anchor))[0]
            whole_rows = gather_tp(late, tp_count, {half_turn: far}).astype(jnp.float32)
            normed_in = rms_norm(whole_rows, pre_gain).astype(jnp.bfloat16)
        source = source if relay else normed_in
        outgoing = jnp.dot(
            dispatch.astype(jnp.bfloat16), source, preferred_element_type=jnp.float32
        ).astype(jnp.bfloat16)
        outgoing = outgoing.reshape(req_count, chunk_items, source.shape[1])
        pieces = lax.all_to_all(outgoing, "req", split_axis=0, concat_axis=0, tiled=True)
        sources, items, widths = pieces.shape
        flat_rows = pieces.reshape(sources * items, widths)
        if relay:
            anchor = flat_rows
            if far is not None:
                raw_rows = gather_pair_tp(flat_rows, col_part, tp_count)
            else:
                raw_rows = gather_tp(flat_rows, tp_count)
            flat_rows = rms_norm(raw_rows.astype(jnp.float32), pre_gain).astype(jnp.bfloat16)
        gate_val = jnp.dot(flat_rows, gate_weight[0], preferred_element_type=jnp.float32)
        up_val = jnp.dot(flat_rows, up_weight[0], preferred_element_type=jnp.float32)
        activ = (jax.nn.silu(gate_val) * up_val).astype(jnp.bfloat16)
        summed = down_scatter_sum_tp(activ, down_weight[0], tp_count)
        summed = summed.reshape(sources, items, col_part)
        back = lax.all_to_all(summed, "req", split_axis=0, concat_axis=0, tiled=True)
        returned.append(back.reshape(req_count * chunk_items, col_part))
    weight_hi = route_weights.astype(jnp.bfloat16)
    weight_lo = (route_weights - weight_hi.astype(jnp.float32)).astype(jnp.bfloat16)
    total_stream = stream
    for c in range(CHUNKS):
        combine_hi = jnp.zeros((row_count, req_count * chunk_items), jnp.bfloat16)
        combine_lo = jnp.zeros((row_count, req_count * chunk_items), jnp.bfloat16)
        for k in range(top):
            hit = (chunk_pairs[:, k][:, None] == slot_ids[None, :]) & (owner_pairs[:, k][:, None] == c)
            combine_hi = jnp.where(hit, weight_hi[:, k][:, None], combine_hi)
            combine_lo = jnp.where(hit, weight_lo[:, k][:, None], combine_lo)
        mixed = jnp.dot(combine_hi, returned[c], preferred_element_type=jnp.float32)
        mixed = mixed + jnp.dot(combine_lo, returned[c], preferred_element_type=jnp.float32)
        total_stream = total_stream + mixed
    out_sums = sum_tp(jnp.sum(total_stream * total_stream, axis=1), tp_count)
    normed_out = (
        total_stream * lax.rsqrt(out_sums / full_width + epsilon)[:, None] * out_gain[None, :]
    )
    return (total_stream.astype(jnp.bfloat16), normed_out.astype(jnp.bfloat16))


def solution(mesh):
    return jax.shard_map(
        shards,
        mesh=mesh,
        in_specs=(
            P("req", "tp"),
            P("req", None),
            P("req", None),
            P(),
            P("tp"),
            P("req", None, "tp"),
            P("req", None, "tp"),
            P("req", "tp", None),
        ),
        out_specs=(P("req", "tp"), P("req", "tp")),
        check_vma=False,
    )
```

```python
import jax
import jax.numpy as jnp
from jax import lax
from jax.sharding import PartitionSpec as P

E = 8
CAP = 128
CHUNKS = 2


epsilon = 1e-05


def rms_norm(values, gain):
    meansq = jnp.mean(values * values, axis=1, keepdims=True)
    return values * lax.rsqrt(meansq + epsilon) * gain[None, :]


def shift_tp(value, step, tp_count):
    return lax.ppermute(value, "tp", [(j, (j + step) % tp_count) for j in range(tp_count)])


def by_source(value, tp_count):
    me = lax.axis_index("tp")
    parts = [value] + [shift_tp(value, s, tp_count) for s in range(1, tp_count)]
    stacked = jnp.stack(parts)
    return jnp.take(stacked, (me - jnp.arange(tp_count)) % tp_count, axis=0)


def gather_tp(value, tp_count, known=None):
    me = lax.axis_index("tp")
    rows, cols = value.shape
    whole = jnp.zeros((rows, tp_count * cols), value.dtype)
    for s in range(tp_count):
        part = (known or {}).get(s)
        if part is None:
            part = value if s == 0 else shift_tp(value, s, tp_count)
        whole = lax.dynamic_update_slice_in_dim(whole, part, ((me - s) % tp_count) * cols, axis=1)
    return whole


def gather_pair_tp(pair, cols, tp_count):
    me = lax.axis_index("tp")
    own = pair[:, :cols]
    parts = {0: own, 2: pair[:, cols:], 1: shift_tp(own, 1, tp_count), 3: shift_tp(own, 3, tp_count)}
    whole = jnp.zeros((pair.shape[0], tp_count * cols), pair.dtype)
    for s, part in parts.items():
        whole = lax.dynamic_update_slice_in_dim(whole, part, ((me - s) % tp_count) * cols, axis=1)
    return whole


def sum_tp(value, tp_count):
    ordered = by_source(value, tp_count)
    total = ordered[0]
    for s in range(1, tp_count):
        total = total + ordered[s]
    return total


def down_scatter_sum_tp(activ, w_down, tp_count):
    me = lax.axis_index("tp")
    width = w_down.shape[1] // tp_count
    terms = []
    for s in list(range(1, tp_count)) + [0]:
        w_block = lax.dynamic_slice_in_dim(w_down, ((me + s) % tp_count) * width, width, axis=1)
        block = jnp.dot(activ, w_block, preferred_element_type=jnp.float32).astype(jnp.bfloat16)
        terms.append(block if s == 0 else shift_tp(block, s, tp_count))
    total = terms[0].astype(jnp.float32)
    for term in terms[1:]:
        total = total + term.astype(jnp.float32)
    return total.astype(jnp.bfloat16)


def shards(hidden, routes, route_weights, pre_gain, out_gain, gate_weight, up_weight, down_weight):
    row_count, col_part = hidden.shape
    tp_count = lax.axis_size("tp")
    req_count = lax.axis_size("req")
    full_width = col_part * tp_count
    copies = req_count // E
    slot_count = CAP // copies
    chunk_items = slot_count // CHUNKS
    stream = hidden.astype(jnp.float32)
    me = lax.axis_index("tp")
    half_turn = tp_count // 2
    far = shift_tp(hidden, half_turn, tp_count) if tp_count == 4 else None
    whole_rows = gather_tp(hidden, tp_count, {half_turn: far}).astype(jnp.float32)
    normed_in = rms_norm(whole_rows, pre_gain).astype(jnp.bfloat16)
    top = routes.shape[1]
    chosen = routes.reshape(-1)
    onehot = (chosen[:, None] == jnp.arange(E, dtype=jnp.int32)[None, :]).astype(jnp.int32)
    slot_rank = jnp.sum((jnp.cumsum(onehot, axis=0) - 1) * onehot, axis=1)
    dest = (slot_rank % copies) * E + chosen
    item = slot_rank // copies
    chunk_of = item // chunk_items
    in_chunk = dest * chunk_items + item % chunk_items
    chunk_pairs = in_chunk.reshape(row_count, top)
    owner_pairs = chunk_of.reshape(row_count, top)
    slot_ids = jnp.arange(req_count * chunk_items, dtype=jnp.int32)
    returned = []
    for c in range(CHUNKS):
        dispatch = jnp.zeros((req_count * chunk_items, row_count), jnp.bool_)
        for k in range(top):
            hit = (slot_ids[:, None] == chunk_pairs[None, :, k]) & (owner_pairs[None, :, k] == c)
            dispatch = dispatch | hit
        relay = True
        source = hidden if far is None else jnp.concatenate([hidden, far], axis=1)
        source = source if relay else normed_in
        outgoing = jnp.dot(
            dispatch.astype(jnp.bfloat16), source, preferred_element_type=jnp.float32
        ).astype(jnp.bfloat16)
        outgoing = outgoing.reshape(req_count, chunk_items, source.shape[1])
        pieces = lax.all_to_all(outgoing, "req", split_axis=0, concat_axis=0, tiled=True)
        sources, items, widths = pieces.shape
        flat_rows = pieces.reshape(sources * items, widths)
        if relay:
            if far is not None:
                raw_rows = gather_pair_tp(flat_rows, col_part, tp_count)
            else:
                raw_rows = gather_tp(flat_rows, tp_count)
            flat_rows = rms_norm(raw_rows.astype(jnp.float32), pre_gain).astype(jnp.bfloat16)
        gate_val = jnp.dot(flat_rows, gate_weight[0], preferred_element_type=jnp.float32)
        up_val = jnp.dot(flat_rows, up_weight[0], preferred_element_type=jnp.float32)
        activ = (jax.nn.silu(gate_val) * up_val).astype(jnp.bfloat16)
        summed = down_scatter_sum_tp(activ, down_weight[0], tp_count)
        summed = summed.reshape(sources, items, col_part)
        back = lax.all_to_all(summed, "req", split_axis=0, concat_axis=0, tiled=True)
        returned.append(back.reshape(req_count * chunk_items, col_part))
    weight_hi = route_weights.astype(jnp.bfloat16)
    weight_lo = (route_weights - weight_hi.astype(jnp.float32)).astype(jnp.bfloat16)
    total_stream = stream
    for c in range(CHUNKS):
        combine_hi = jnp.zeros((row_count, req_count * chunk_items), jnp.bfloat16)
        combine_lo = jnp.zeros((row_count, req_count * chunk_items), jnp.bfloat16)
        for k in range(top):
            hit = (chunk_pairs[:, k][:, None] == slot_ids[None, :]) & (owner_pairs[:, k][:, None] == c)
            combine_hi = jnp.where(hit, weight_hi[:, k][:, None], combine_hi)
            combine_lo = jnp.where(hit, weight_lo[:, k][:, None], combine_lo)
        mixed = jnp.dot(combine_hi, returned[c], preferred_element_type=jnp.float32)
        mixed = mixed + jnp.dot(combine_lo, returned[c], preferred_element_type=jnp.float32)
        total_stream = total_stream + mixed
    out_sums = sum_tp(jnp.sum(total_stream * total_stream, axis=1), tp_count)
    normed_out = (
        total_stream * lax.rsqrt(out_sums / full_width + epsilon)[:, None] * out_gain[None, :]
    )
    return (total_stream.astype(jnp.bfloat16), normed_out.astype(jnp.bfloat16))


def solution(mesh):
    return jax.shard_map(
        shards,
        mesh=mesh,
        in_specs=(
            P("req", "tp"),
            P("req", None),
            P("req", None),
            P(),
            P("tp"),
            P("req", None, "tp"),
            P("req", None, "tp"),
            P("req", "tp", None),
        ),
        out_specs=(P("req", "tp"), P("req", "tp")),
        check_vma=False,
    )
```

```python
import jax
import jax.numpy as jnp
from jax import lax
from jax.sharding import PartitionSpec as P

E = 8
CAP = 128
CHUNKS = 2


epsilon = 1e-05


def rms_norm(values, gain):
    meansq = jnp.mean(values * values, axis=1, keepdims=True)
    return values * lax.rsqrt(meansq + epsilon) * gain[None, :]


def shift_tp(value, step, tp_count):
    return lax.ppermute(value, "tp", [(j, (j + step) % tp_count) for j in range(tp_count)])


def by_source(value, tp_count):
    me = lax.axis_index("tp")
    parts = [value] + [shift_tp(value, s, tp_count) for s in range(1, tp_count)]
    stacked = jnp.stack(parts)
    return jnp.take(stacked, (me - jnp.arange(tp_count)) % tp_count, axis=0)


def gather_tp(value, tp_count, known=None):
    me = lax.axis_index("tp")
    rows, cols = value.shape
    whole = jnp.zeros((rows, tp_count * cols), value.dtype)
    for s in range(tp_count):
        part = (known or {}).get(s)
        if part is None:
            part = value if s == 0 else shift_tp(value, s, tp_count)
        whole = lax.dynamic_update_slice_in_dim(whole, part, ((me - s) % tp_count) * cols, axis=1)
    return whole


def gather_pair_tp(pair, cols, tp_count):
    me = lax.axis_index("tp")
    own = pair[:, :cols]
    parts = {0: own, 2: pair[:, cols:], 1: shift_tp(own, 1, tp_count), 3: shift_tp(own, 3, tp_count)}
    whole = jnp.zeros((pair.shape[0], tp_count * cols), pair.dtype)
    for s, part in parts.items():
        whole = lax.dynamic_update_slice_in_dim(whole, part, ((me - s) % tp_count) * cols, axis=1)
    return whole


def sum_tp(value, tp_count):
    spread = jnp.broadcast_to(value[None], (tp_count,) + value.shape)
    ordered = lax.all_to_all(spread, "tp", 0, 0, tiled=True)
    total = ordered[0]
    for s in range(1, tp_count):
        total = total + ordered[s]
    return total


def down_scatter_sum_tp(activ, w_down, tp_count):
    me = lax.axis_index("tp")
    width = w_down.shape[1] // tp_count
    terms = []
    for s in list(range(1, tp_count)) + [0]:
        w_block = lax.dynamic_slice_in_dim(w_down, ((me + s) % tp_count) * width, width, axis=1)
        block = jnp.dot(activ, w_block, preferred_element_type=jnp.float32).astype(jnp.bfloat16)
        terms.append(block if s == 0 else shift_tp(block, s, tp_count))
    total = terms[0].astype(jnp.float32)
    for term in terms[1:]:
        total = total + term.astype(jnp.float32)
    return total.astype(jnp.bfloat16)


def shards(hidden, routes, route_weights, pre_gain, out_gain, gate_weight, up_weight, down_weight):
    row_count, col_part = hidden.shape
    tp_count = lax.axis_size("tp")
    req_count = lax.axis_size("req")
    full_width = col_part * tp_count
    copies = req_count // E
    slot_count = CAP // copies
    chunk_items = slot_count // CHUNKS
    stream = hidden.astype(jnp.float32)
    me = lax.axis_index("tp")
    half_turn = tp_count // 2
    far = shift_tp(hidden, half_turn, tp_count) if tp_count == 4 else None
    whole_rows = gather_tp(hidden, tp_count, {half_turn: far}).astype(jnp.float32)
    normed_in = rms_norm(whole_rows, pre_gain).astype(jnp.bfloat16)
    top = routes.shape[1]
    chosen = routes.reshape(-1)
    onehot = (chosen[:, None] == jnp.arange(E, dtype=jnp.int32)[None, :]).astype(jnp.int32)
    slot_rank = jnp.sum((jnp.cumsum(onehot, axis=0) - 1) * onehot, axis=1)
    dest = (slot_rank % copies) * E + chosen
    item = slot_rank // copies
    chunk_of = item // chunk_items
    in_chunk = dest * chunk_items + item % chunk_items
    chunk_pairs = in_chunk.reshape(row_count, top)
    owner_pairs = chunk_of.reshape(row_count, top)
    slot_ids = jnp.arange(req_count * chunk_items, dtype=jnp.int32)
    returned = []
    for c in range(CHUNKS):
        dispatch = jnp.zeros((req_count * chunk_items, row_count), jnp.bool_)
        for k in range(top):
            hit = (slot_ids[:, None] == chunk_pairs[None, :, k]) & (owner_pairs[None, :, k] == c)
            dispatch = dispatch | hit
        relay = c == 0
        source = hidden if far is None else jnp.concatenate([hidden, far], axis=1)
        source = source if relay else normed_in
        outgoing = jnp.dot(
            dispatch.astype(jnp.bfloat16), source, preferred_element_type=jnp.float32
        ).astype(jnp.bfloat16)
        outgoing = outgoing.reshape(req_count, chunk_items, source.shape[1])
        pieces = lax.all_to_all(outgoing, "req", split_axis=0, concat_axis=0, tiled=True)
        sources, items, widths = pieces.shape
        flat_rows = pieces.reshape(sources * items, widths)
        if relay:
            if far is not None:
                raw_rows = gather_pair_tp(flat_rows, col_part, tp_count)
            else:
                raw_rows = gather_tp(flat_rows, tp_count)
            flat_rows = rms_norm(raw_rows.astype(jnp.float32), pre_gain).astype(jnp.bfloat16)
        gate_val = jnp.dot(flat_rows, gate_weight[0], preferred_element_type=jnp.float32)
        up_val = jnp.dot(flat_rows, up_weight[0], preferred_element_type=jnp.float32)
        activ = (jax.nn.silu(gate_val) * up_val).astype(jnp.bfloat16)
        summed = down_scatter_sum_tp(activ, down_weight[0], tp_count)
        summed = summed.reshape(sources, items, col_part)
        back = lax.all_to_all(summed, "req", split_axis=0, concat_axis=0, tiled=True)
        returned.append(back.reshape(req_count * chunk_items, col_part))
    weight_hi = route_weights.astype(jnp.bfloat16)
    weight_lo = (route_weights - weight_hi.astype(jnp.float32)).astype(jnp.bfloat16)
    total_stream = stream
    for c in range(CHUNKS):
        combine_hi = jnp.zeros((row_count, req_count * chunk_items), jnp.bfloat16)
        combine_lo = jnp.zeros((row_count, req_count * chunk_items), jnp.bfloat16)
        for k in range(top):
            hit = (chunk_pairs[:, k][:, None] == slot_ids[None, :]) & (owner_pairs[:, k][:, None] == c)
            combine_hi = jnp.where(hit, weight_hi[:, k][:, None], combine_hi)
            combine_lo = jnp.where(hit, weight_lo[:, k][:, None], combine_lo)
        mixed = jnp.dot(combine_hi, returned[c], preferred_element_type=jnp.float32)
        mixed = mixed + jnp.dot(combine_lo, returned[c], preferred_element_type=jnp.float32)
        total_stream = total_stream + mixed
    out_sums = sum_tp(jnp.sum(total_stream * total_stream, axis=1), tp_count)
    normed_out = (
        total_stream * lax.rsqrt(out_sums / full_width + epsilon)[:, None] * out_gain[None, :]
    )
    return (total_stream.astype(jnp.bfloat16), normed_out.astype(jnp.bfloat16))


def solution(mesh):
    return jax.shard_map(
        shards,
        mesh=mesh,
        in_specs=(
            P("req", "tp"),
            P("req", None),
            P("req", None),
            P(),
            P("tp"),
            P("req", None, "tp"),
            P("req", None, "tp"),
            P("req", "tp", None),
        ),
        out_specs=(P("req", "tp"), P("req", "tp")),
        check_vma=False,
    )
```

```python
import jax
import jax.numpy as jnp
from jax import lax
from jax.sharding import PartitionSpec as P

E = 8
CAP = 128
CHUNKS = 2


epsilon = 1e-05


def rms_norm(values, gain):
    meansq = jnp.mean(values * values, axis=1, keepdims=True)
    return values * lax.rsqrt(meansq + epsilon) * gain[None, :]


def shift_tp(value, step, tp_count):
    return lax.ppermute(value, "tp", [(j, (j + step) % tp_count) for j in range(tp_count)])


def by_source(value, tp_count):
    me = lax.axis_index("tp")
    parts = [value] + [shift_tp(value, s, tp_count) for s in range(1, tp_count)]
    stacked = jnp.stack(parts)
    return jnp.take(stacked, (me - jnp.arange(tp_count)) % tp_count, axis=0)


def gather_tp(value, tp_count, known=None):
    me = lax.axis_index("tp")
    rows, cols = value.shape
    whole = jnp.zeros((rows, tp_count * cols), value.dtype)
    for s in range(tp_count):
        part = (known or {}).get(s)
        if part is None:
            part = value if s == 0 else shift_tp(value, s, tp_count)
        whole = lax.dynamic_update_slice_in_dim(whole, part, ((me - s) % tp_count) * cols, axis=1)
    return whole


def gather_pair_tp(pair, cols, tp_count):
    me = lax.axis_index("tp")
    own = pair[:, :cols]
    parts = {0: own, 2: pair[:, cols:], 1: shift_tp(own, 1, tp_count), 3: shift_tp(own, 3, tp_count)}
    whole = jnp.zeros((pair.shape[0], tp_count * cols), pair.dtype)
    for s, part in parts.items():
        whole = lax.dynamic_update_slice_in_dim(whole, part, ((me - s) % tp_count) * cols, axis=1)
    return whole


def sum_tp(value, tp_count):
    total = value
    for s in range(1, tp_count):
        total = total + shift_tp(value, s, tp_count)
    return total


def down_scatter_sum_tp(activ, w_down, tp_count):
    me = lax.axis_index("tp")
    width = w_down.shape[1] // tp_count
    terms = []
    for s in list(range(1, tp_count)) + [0]:
        w_block = lax.dynamic_slice_in_dim(w_down, ((me + s) % tp_count) * width, width, axis=1)
        block = jnp.dot(activ, w_block, preferred_element_type=jnp.float32).astype(jnp.bfloat16)
        terms.append(block if s == 0 else shift_tp(block, s, tp_count))
    total = terms[0].astype(jnp.float32)
    for term in terms[1:]:
        total = total + term.astype(jnp.float32)
    return total.astype(jnp.bfloat16)


def shards(hidden, routes, route_weights, pre_gain, out_gain, gate_weight, up_weight, down_weight):
    row_count, col_part = hidden.shape
    tp_count = lax.axis_size("tp")
    req_count = lax.axis_size("req")
    full_width = col_part * tp_count
    copies = req_count // E
    slot_count = CAP // copies
    chunk_items = slot_count // CHUNKS
    stream = hidden.astype(jnp.float32)
    me = lax.axis_index("tp")
    half_turn = tp_count // 2
    far = shift_tp(hidden, half_turn, tp_count) if tp_count == 4 else None
    whole_rows = gather_tp(hidden, tp_count, {half_turn: far}).astype(jnp.float32)
    normed_in = rms_norm(whole_rows, pre_gain).astype(jnp.bfloat16)
    top = routes.shape[1]
    chosen = routes.reshape(-1)
    onehot = (chosen[:, None] == jnp.arange(E, dtype=jnp.int32)[None, :]).astype(jnp.int32)
    slot_rank = jnp.sum((jnp.cumsum(onehot, axis=0) - 1) * onehot, axis=1)
    dest = (slot_rank % copies) * E + chosen
    item = slot_rank // copies
    chunk_of = item // chunk_items
    in_chunk = dest * chunk_items + item % chunk_items
    chunk_pairs = in_chunk.reshape(row_count, top)
    owner_pairs = chunk_of.reshape(row_count, top)
    slot_ids = jnp.arange(req_count * chunk_items, dtype=jnp.int32)
    returned = []
    for c in range(CHUNKS):
        dispatch = jnp.zeros((req_count * chunk_items, row_count), jnp.bool_)
        for k in range(top):
            hit = (slot_ids[:, None] == chunk_pairs[None, :, k]) & (owner_pairs[None, :, k] == c)
            dispatch = dispatch | hit
        relay = c == 0
        source = hidden if far is None else jnp.concatenate([hidden, far], axis=1)
        source = source if relay else normed_in
        outgoing = jnp.dot(
            dispatch.astype(jnp.bfloat16), source, preferred_element_type=jnp.float32
        ).astype(jnp.bfloat16)
        outgoing = outgoing.reshape(req_count, chunk_items, source.shape[1])
        pieces = lax.all_to_all(outgoing, "req", split_axis=0, concat_axis=0, tiled=True)
        sources, items, widths = pieces.shape
        flat_rows = pieces.reshape(sources * items, widths)
        if relay:
            if far is not None:
                raw_rows = gather_pair_tp(flat_rows, col_part, tp_count)
            else:
                raw_rows = gather_tp(flat_rows, tp_count)
            flat_rows = rms_norm(raw_rows.astype(jnp.float32), pre_gain).astype(jnp.bfloat16)
        gate_val = jnp.dot(flat_rows, gate_weight[0], preferred_element_type=jnp.float32)
        up_val = jnp.dot(flat_rows, up_weight[0], preferred_element_type=jnp.float32)
        activ = (jax.nn.silu(gate_val) * up_val).astype(jnp.bfloat16)
        summed = down_scatter_sum_tp(activ, down_weight[0], tp_count)
        summed = summed.reshape(sources, items, col_part)
        back = lax.all_to_all(summed, "req", split_axis=0, concat_axis=0, tiled=True)
        returned.append(back.reshape(req_count * chunk_items, col_part))
    weight_hi = route_weights.astype(jnp.bfloat16)
    weight_lo = (route_weights - weight_hi.astype(jnp.float32)).astype(jnp.bfloat16)
    total_stream = stream
    for c in range(CHUNKS):
        combine_hi = jnp.zeros((row_count, req_count * chunk_items), jnp.bfloat16)
        combine_lo = jnp.zeros((row_count, req_count * chunk_items), jnp.bfloat16)
        for k in range(top):
            hit = (chunk_pairs[:, k][:, None] == slot_ids[None, :]) & (owner_pairs[:, k][:, None] == c)
            combine_hi = jnp.where(hit, weight_hi[:, k][:, None], combine_hi)
            combine_lo = jnp.where(hit, weight_lo[:, k][:, None], combine_lo)
        mixed = jnp.dot(combine_hi, returned[c], preferred_element_type=jnp.float32)
        mixed = mixed + jnp.dot(combine_lo, returned[c], preferred_element_type=jnp.float32)
        total_stream = total_stream + mixed
    out_sums = sum_tp(jnp.sum(total_stream * total_stream, axis=1), tp_count)
    normed_out = (
        total_stream * lax.rsqrt(out_sums / full_width + epsilon)[:, None] * out_gain[None, :]
    )
    return (total_stream.astype(jnp.bfloat16), normed_out.astype(jnp.bfloat16))


def solution(mesh):
    return jax.shard_map(
        shards,
        mesh=mesh,
        in_specs=(
            P("req", "tp"),
            P("req", None),
            P("req", None),
            P(),
            P("tp"),
            P("req", None, "tp"),
            P("req", None, "tp"),
            P("req", "tp", None),
        ),
        out_specs=(P("req", "tp"), P("req", "tp")),
        check_vma=False,
    )
```

```python
import jax
import jax.numpy as jnp
from jax import lax
from jax.sharding import PartitionSpec as P

E = 8
CAP = 128
CHUNKS = 2


epsilon = 1e-05


def rms_norm(values, gain):
    meansq = jnp.mean(values * values, axis=1, keepdims=True)
    return values * lax.rsqrt(meansq + epsilon) * gain[None, :]


def shift_tp(value, step, tp_count):
    return lax.ppermute(value, "tp", [(j, (j + step) % tp_count) for j in range(tp_count)])


def by_source(value, tp_count):
    me = lax.axis_index("tp")
    parts = [value] + [shift_tp(value, s, tp_count) for s in range(1, tp_count)]
    stacked = jnp.stack(parts)
    return jnp.take(stacked, (me - jnp.arange(tp_count)) % tp_count, axis=0)


def gather_tp(value, tp_count, known=None):
    me = lax.axis_index("tp")
    rows, cols = value.shape
    whole = jnp.zeros((rows, tp_count * cols), value.dtype)
    for s in range(tp_count):
        part = (known or {}).get(s)
        if part is None:
            part = value if s == 0 else shift_tp(value, s, tp_count)
        whole = lax.dynamic_update_slice_in_dim(whole, part, ((me - s) % tp_count) * cols, axis=1)
    return whole


def gather_pair_tp(pair, cols, tp_count):
    me = lax.axis_index("tp")
    own = pair[:, :cols]
    parts = {0: own, 2: pair[:, cols:], 1: shift_tp(own, 1, tp_count), 3: shift_tp(own, 3, tp_count)}
    whole = jnp.zeros((pair.shape[0], tp_count * cols), pair.dtype)
    for s, part in parts.items():
        whole = lax.dynamic_update_slice_in_dim(whole, part, ((me - s) % tp_count) * cols, axis=1)
    return whole


def sum_tp(value, tp_count):
    total = value
    for s in range(1, tp_count):
        total = total + shift_tp(value, s, tp_count)
    return total


def down_scatter_sum_tp(activ, w_down, tp_count):
    me = lax.axis_index("tp")
    width = w_down.shape[1] // tp_count
    terms = []
    far_first = [tp_count // 2] + [s for s in range(1, tp_count) if s != tp_count // 2]
    for s in far_first + [0]:
        w_block = lax.dynamic_slice_in_dim(w_down, ((me + s) % tp_count) * width, width, axis=1)
        block = jnp.dot(activ, w_block, preferred_element_type=jnp.float32).astype(jnp.bfloat16)
        terms.append(block if s == 0 else shift_tp(block, s, tp_count))
    total = terms[0].astype(jnp.float32)
    for term in terms[1:]:
        total = total + term.astype(jnp.float32)
    return total.astype(jnp.bfloat16)


def shards(hidden, routes, route_weights, pre_gain, out_gain, gate_weight, up_weight, down_weight):
    row_count, col_part = hidden.shape
    tp_count = lax.axis_size("tp")
    req_count = lax.axis_size("req")
    full_width = col_part * tp_count
    copies = req_count // E
    slot_count = CAP // copies
    chunk_items = slot_count // CHUNKS
    stream = hidden.astype(jnp.float32)
    me = lax.axis_index("tp")
    half_turn = tp_count // 2
    far = shift_tp(hidden, half_turn, tp_count) if tp_count == 4 else None
    whole_rows = gather_tp(hidden, tp_count, {half_turn: far}).astype(jnp.float32)
    normed_in = rms_norm(whole_rows, pre_gain).astype(jnp.bfloat16)
    top = routes.shape[1]
    chosen = routes.reshape(-1)
    onehot = (chosen[:, None] == jnp.arange(E, dtype=jnp.int32)[None, :]).astype(jnp.int32)
    slot_rank = jnp.sum((jnp.cumsum(onehot, axis=0) - 1) * onehot, axis=1)
    dest = (slot_rank % copies) * E + chosen
    item = slot_rank // copies
    chunk_of = item // chunk_items
    in_chunk = dest * chunk_items + item % chunk_items
    chunk_pairs = in_chunk.reshape(row_count, top)
    owner_pairs = chunk_of.reshape(row_count, top)
    slot_ids = jnp.arange(req_count * chunk_items, dtype=jnp.int32)
    returned = []
    for c in range(CHUNKS):
        dispatch = jnp.zeros((req_count * chunk_items, row_count), jnp.bool_)
        for k in range(top):
            hit = (slot_ids[:, None] == chunk_pairs[None, :, k]) & (owner_pairs[None, :, k] == c)
            dispatch = dispatch | hit
        relay = c == 0
        source = hidden if far is None else jnp.concatenate([hidden, far], axis=1)
        source = source if relay else normed_in
        outgoing = jnp.dot(
            dispatch.astype(jnp.bfloat16), source, preferred_element_type=jnp.float32
        ).astype(jnp.bfloat16)
        outgoing = outgoing.reshape(req_count, chunk_items, source.shape[1])
        pieces = lax.all_to_all(outgoing, "req", split_axis=0, concat_axis=0, tiled=True)
        sources, items, widths = pieces.shape
        flat_rows = pieces.reshape(sources * items, widths)
        if relay:
            if far is not None:
                raw_rows = gather_pair_tp(flat_rows, col_part, tp_count)
            else:
                raw_rows = gather_tp(flat_rows, tp_count)
            flat_rows = rms_norm(raw_rows.astype(jnp.float32), pre_gain).astype(jnp.bfloat16)
        gate_val = jnp.dot(flat_rows, gate_weight[0], preferred_element_type=jnp.float32)
        up_val = jnp.dot(flat_rows, up_weight[0], preferred_element_type=jnp.float32)
        activ = (jax.nn.silu(gate_val) * up_val).astype(jnp.bfloat16)
        summed = down_scatter_sum_tp(activ, down_weight[0], tp_count)
        summed = summed.reshape(sources, items, col_part)
        back = lax.all_to_all(summed, "req", split_axis=0, concat_axis=0, tiled=True)
        returned.append(back.reshape(req_count * chunk_items, col_part))
    weight_hi = route_weights.astype(jnp.bfloat16)
    weight_lo = (route_weights - weight_hi.astype(jnp.float32)).astype(jnp.bfloat16)
    total_stream = stream
    for c in range(CHUNKS):
        combine_hi = jnp.zeros((row_count, req_count * chunk_items), jnp.bfloat16)
        combine_lo = jnp.zeros((row_count, req_count * chunk_items), jnp.bfloat16)
        for k in range(top):
            hit = (chunk_pairs[:, k][:, None] == slot_ids[None, :]) & (owner_pairs[:, k][:, None] == c)
            combine_hi = jnp.where(hit, weight_hi[:, k][:, None], combine_hi)
            combine_lo = jnp.where(hit, weight_lo[:, k][:, None], combine_lo)
        mixed = jnp.dot(combine_hi, returned[c], preferred_element_type=jnp.float32)
        mixed = mixed + jnp.dot(combine_lo, returned[c], preferred_element_type=jnp.float32)
        total_stream = total_stream + mixed
    out_sums = sum_tp(jnp.sum(total_stream * total_stream, axis=1), tp_count)
    normed_out = (
        total_stream * lax.rsqrt(out_sums / full_width + epsilon)[:, None] * out_gain[None, :]
    )
    return (total_stream.astype(jnp.bfloat16), normed_out.astype(jnp.bfloat16))


def solution(mesh):
    return jax.shard_map(
        shards,
        mesh=mesh,
        in_specs=(
            P("req", "tp"),
            P("req", None),
            P("req", None),
            P(),
            P("tp"),
            P("req", None, "tp"),
            P("req", None, "tp"),
            P("req", "tp", None),
        ),
        out_specs=(P("req", "tp"), P("req", "tp")),
        check_vma=False,
    )
```
